512 devices in a mesh: dp: 32 (over z, x_lo, core), tensor: 16 (over y, x_hi).
Axes of the slice: x: 4 (x_hi: 2, x_lo: 2; x = x_hi * 2 + x_lo), y: 8, z: 8, core: 2. Of those that a mesh axis runs over, the one named last changes fastest.
Arguments:
- features: bfloat16 [5120, 36864], P('tensor', 'dp'), may hold values from -24 to 24
- cotangents: bfloat16 [36864, 2048], P('dp', 'tensor'), may hold values from -24 to 24
- labels: int32 [36864], P('dp'), may hold values from 0 to 2
- diff_mask: int32 [36864], P('dp'), may hold values 0 or 1
- class_weight: float32 [3], replicated, may hold values from 0.25 to 2
- owners: int32 [16, 32], P('tensor'), may hold values from 0 to 31, each once within a row
- momentum: float32 [5120, 2048], P('dp', 'tensor'), may hold values from -3 to 3
Outputs:
- update: bfloat16 [5120, 2048], P(None, 'tensor')
- new_momentum: float32 [5120, 2048], P('dp', 'tensor')
The draws below stay inside these ranges and needn't reach their ends.
Inputs may be any that keep to these rules, and one draw needn't show every extreme that they name: `owners`: each row names every dp index once.
All inputs are finite; a program needn't handle non-finite values. No bound on the sum of `diff_mask` on one device may be relied on, other than what follows from the above.
Results may differ from the reference program's by a relative error of at most 0.0065.
Values may be sent and summed in bfloat16 or wider, within the bound.
No kernel may reach another device: no remote copies, remote signals or barrier semaphores. Data moves between devices by JAX's collectives and lax.ppermute only.
A program may use at most 64 MiB of HBM per device.

```python
import math
import jax
import jax.numpy as jnp
from jax import lax

D = 5120
HEAD_DIM = 128
ITERS = 5
HEADS = 16
COLUMNS = 2048
TOKENS = 36864
BLOCK_ROWS = 160
N_DP = 32


def scaled_field(key, rows_count, cols_count, scale_on_rows):
    first, second, third = jax.random.split(key, 3)
    base = jnp.clip(jax.random.normal(first, (rows_count, cols_count), jnp.float32), -4.0, 4.0)
    wide_lo, wide_hi = (math.log(0.3), math.log(3.0))
    if scale_on_rows:
        spread = jnp.exp(jax.random.uniform(second, (rows_count, 1), jnp.float32, wide_lo, wide_hi))
        others = jnp.exp(jax.random.uniform(third, (1, cols_count), jnp.float32, math.log(0.5), math.log(2.0)))
    else:
        spread = jnp.exp(jax.random.uniform(second, (1, cols_count), jnp.float32, wide_lo, wide_hi))
        others = jnp.exp(jax.random.uniform(third, (rows_count, 1), jnp.float32, math.log(0.5), math.log(2.0)))
    return base * spread * others


def draw_features(key, part):
    return scaled_field(jax.random.fold_in(key, 11), D, TOKENS, True).astype(jnp.bfloat16)


def draw_cotangents(key, part):
    return scaled_field(jax.random.fold_in(key, 23), TOKENS, COLUMNS, False).astype(jnp.bfloat16)


def plant(entries, key, low, largest):
    longest = entries.shape.index(max(entries.shape))
    spots = []
    for shift in (0, 1):
        where = [jax.random.randint(jax.random.fold_in(key, axis), (), 0, length) for axis, length in enumerate(entries.shape)]
        where[longest] = (where[longest] + shift) % entries.shape[longest]
        spots.append(tuple(where))
    return entries.at[spots[0]].set(low).at[spots[1]].set(largest)


def shard_levels(key, shape, shards, least, top_value):
    gain, own = 1.0, jax.random.fold_in(key, 6)
    for axis_at, blocks in shards:
        steps = jnp.exp(jax.random.uniform(jax.random.fold_in(own, axis_at), (blocks,), jnp.float32, least / len(shards), top_value / len(shards)))
        gain = gain * jnp.repeat(steps, shape[axis_at] // blocks).reshape([-1 if axis == axis_at else 1 for axis in range(len(shape))])
    return gain


def bell_draw(key, shape, deviation, limit, cuts=(), held_as=jnp.bfloat16):
    drawn = deviation * jax.random.normal(key, shape, jnp.float32)
    if cuts:
        drawn = drawn * shard_levels(key, shape, cuts, -0.22, 0.18)
    return jnp.clip(drawn, -limit, limit).astype(held_as)


def setup_inputs(seed: int = 0) -> dict:
    key_list = jax.random.split(jax.random.key(seed), 8)
    return {
        "features": draw_features(jax.random.fold_in(key_list[7], 71), 0),
        "cotangents": draw_cotangents(jax.random.fold_in(key_list[7], 71), 0),
        "labels": plant(jax.random.randint(key_list[2], (TOKENS,), 0, 3), jax.random.fold_in(key_list[2], 1), 0, 2).astype(jnp.int32),
        "diff_mask": plant((jax.random.randint(key_list[3], (TOKENS,), 0, 2) < 1).astype(jnp.int32), jax.random.fold_in(key_list[3], 1), 0, 1),
        "class_weight": jnp.clip(jnp.exp(jax.random.uniform(key_list[4], (3,), jnp.float32, math.log(0.25), math.log(2.0))), 0.25, 2.0),
        "owners": jax.vmap(lambda own: jax.random.permutation(own, N_DP))(jax.random.split(key_list[5], HEADS)).reshape((HEADS, N_DP)).astype(jnp.int32),
        "momentum": bell_draw(key_list[6], (D, COLUMNS), 0.5, 3.0, ((0, 32), (1, 16)), jnp.float32),
    }


decay_rate = 0.95
quintic_first = 3.4445
quintic_second = -4.775
quintic_third = 2.0315
norm_epsilon = 1e-07

def weigh(cotangents, labels, diff_mask, class_weight, total_tokens):
    classes = jnp.arange(class_weight.shape[0], dtype=jnp.int32)
    picked = (labels[:, None] == classes[None, :]).astype(jnp.float32)
    token_weight = diff_mask.astype(jnp.float32) * lax.optimization_barrier(jnp.sum(picked * class_weight[None, :], axis=1))
    factor = token_weight / math.sqrt(total_tokens)
    return (cotangents.astype(jnp.float32) * factor[:, None]).astype(jnp.bfloat16)

def invert(owners):
    number = owners.shape[1]
    candidates = jnp.arange(number, dtype=jnp.int32)
    matches = owners[:, None, :] == candidates[None, :, None]
    return lax.optimization_barrier(jnp.sum(jnp.where(matches, candidates[None, None, :], 0), axis=2)).astype(jnp.int32)

def reorder(blocks, lookup):
    return jnp.take_along_axis(blocks, jnp.transpose(lookup)[:, None, :, None].astype(jnp.int32), axis=0)

def orthogonalize(nesterov):
    frobenius = jnp.sqrt(lax.optimization_barrier(jnp.sum(nesterov * nesterov, axis=(-3, -1), keepdims=True))) + norm_epsilon
    iterate = nesterov / frobenius
    for step in range(ITERS):
        gram_matrix = jnp.einsum('...rhc,...rhd->...hcd', iterate, iterate, precision=lax.Precision.HIGHEST)
        poly_matrix = quintic_second * gram_matrix + quintic_third * jnp.einsum('...hcd,...hde->...hce', gram_matrix, gram_matrix, precision=lax.Precision.HIGHEST)
        iterate = quintic_first * iterate + jnp.einsum('...rhc,...hcd->...rhd', iterate, poly_matrix, precision=lax.Precision.HIGHEST)
    return iterate

def reference(features, cotangents, labels, diff_mask, class_weight, owners, momentum):
    scaled = weigh(cotangents, labels, diff_mask, class_weight, TOKENS)
    grad = jnp.dot(features, scaled, preferred_element_type=jnp.float32)
    blocks = grad.reshape(N_DP, BLOCK_ROWS, HEADS, HEAD_DIM)
    owned = reorder(blocks, invert(owners))
    previous = momentum.reshape(N_DP, BLOCK_ROWS, HEADS, HEAD_DIM)
    new_momentum = decay_rate * previous + owned
    nesterov = owned + decay_rate * new_momentum
    ortho = orthogonalize(nesterov)
    scaled_update = (ortho * math.sqrt(BLOCK_ROWS)).astype(jnp.bfloat16)
    update = reorder(scaled_update, owners)
    return (update.reshape(D, COLUMNS), new_momentum.reshape(D, COLUMNS))
```

```python
import math

import jax
import jax.numpy as jnp
from jax import lax
from jax.sharding import PartitionSpec as P

ITERS = 5


decay_rate = 0.95
quintic_first = 3.4445
quintic_second = -4.775
quintic_third = 2.0315
norm_epsilon = 1e-07


def weigh(cotangents, labels, diff_mask, class_weight, total_tokens):
    classes = jnp.arange(class_weight.shape[0], dtype=jnp.int32)
    picked = (labels[:, None] == classes[None, :]).astype(jnp.float32)
    token_weight = diff_mask.astype(jnp.float32) * jnp.sum(picked * class_weight[None, :], axis=1)
    factor = token_weight / math.sqrt(total_tokens)
    return (cotangents.astype(jnp.float32) * factor[:, None]).astype(jnp.bfloat16)


def invert(owners):
    number = owners.shape[1]
    candidates = jnp.arange(number, dtype=jnp.int32)
    matches = owners[:, None, :] == candidates[None, :, None]
    return jnp.sum(jnp.where(matches, candidates[None, None, :], 0), axis=2)


def reorder(blocks, lookup):
    return jnp.take_along_axis(blocks, jnp.transpose(lookup)[:, None, :, None], axis=0)


def orthogonalize(nesterov):
    frobenius = jnp.sqrt(jnp.sum(nesterov * nesterov, axis=(-3, -1), keepdims=True)) + norm_epsilon
    iterate = nesterov / frobenius
    for step in range(ITERS):
        gram_matrix = jnp.einsum(
            "...rhc,...rhd->...hcd", iterate, iterate, precision=lax.Precision.HIGHEST
        )
        poly_matrix = quintic_second * gram_matrix + quintic_third * jnp.einsum(
            "...hcd,...hde->...hce", gram_matrix, gram_matrix, precision=lax.Precision.HIGHEST
        )
        iterate = quintic_first * iterate + jnp.einsum(
            "...rhc,...hcd->...rhd", iterate, poly_matrix, precision=lax.Precision.HIGHEST
        )
    return iterate


def shards(features, cotangents, labels, diff_mask, class_weight, owners, momentum):
    dp_count = lax.axis_size("dp")
    tensor_count = lax.axis_size("tensor")
    local_tokens = cotangents.shape[0]
    scaled = weigh(cotangents, labels, diff_mask, class_weight, local_tokens * dp_count)
    heads_here = owners.shape[0]
    head_width = cotangents.shape[1] // heads_here
    block_rows = features.shape[0] * tensor_count // dp_count
    inverse = invert(owners)
    partial_grad = jnp.dot(
        lax.all_gather(features, "tensor", axis=0, tiled=True),
        scaled,
        preferred_element_type=jnp.float32,
    )
    blocks = partial_grad.reshape(dp_count, block_rows, heads_here * head_width)
    in_owner_order = jnp.take(blocks, inverse[0], axis=0).reshape(dp_count * block_rows, heads_here * head_width)
    own_block = lax.psum_scatter(in_owner_order, "dp", scatter_dimension=0, tiled=True).reshape(
        block_rows, heads_here, head_width
    )
    previous = momentum.reshape(block_rows, heads_here, head_width)
    new_momentum = decay_rate * previous + own_block
    nesterov = own_block + decay_rate * new_momentum
    ortho = orthogonalize(nesterov)
    own_update = (
        (ortho * math.sqrt(block_rows))
        .astype(jnp.bfloat16)
        .reshape(block_rows, heads_here * head_width)
    )
    gathered = lax.all_gather(own_update, "dp", axis=0, tiled=True)
    placed = reorder(gathered.reshape(dp_count, block_rows, heads_here, head_width), owners)
    return (
        placed.reshape(dp_count * block_rows, heads_here * head_width),
        new_momentum.reshape(block_rows, heads_here * head_width),
    )


def solution(mesh):
    in_specs = (
        P("tensor", "dp"),
        P("dp", "tensor"),
        P("dp"),
        P("dp"),
        P(),
        P("tensor", None),
        P("dp", "tensor"),
    )
    out_specs = (P(None, "tensor"), P("dp", "tensor"))
    return jax.shard_map(shards, mesh=mesh, in_specs=in_specs, out_specs=out_specs, check_vma=False)
```

```python
import math

import jax
import jax.numpy as jnp
from jax import lax
from jax.sharding import PartitionSpec as P

ITERS = 5


decay_rate = 0.95
quintic_first = 3.4445
quintic_second = -4.775
quintic_third = 2.0315
norm_epsilon = 1e-07


def weigh(cotangents, labels, diff_mask, class_weight, total_tokens):
    classes = jnp.arange(class_weight.shape[0], dtype=jnp.int32)
    picked = (labels[:, None] == classes[None, :]).astype(jnp.float32)
    token_weight = diff_mask.astype(jnp.float32) * jnp.sum(picked * class_weight[None, :], axis=1)
    factor = token_weight / math.sqrt(total_tokens)
    return (cotangents.astype(jnp.float32) * factor[:, None]).astype(jnp.bfloat16)


def invert(owners):
    number = owners.shape[1]
    candidates = jnp.arange(number, dtype=jnp.int32)
    matches = owners[:, None, :] == candidates[None, :, None]
    return jnp.sum(jnp.where(matches, candidates[None, None, :], 0), axis=2)


def reorder(blocks, lookup):
    return jnp.take_along_axis(blocks, jnp.transpose(lookup)[:, None, :, None], axis=0)


def orthogonalize(nesterov):
    frobenius = jnp.sqrt(jnp.sum(nesterov * nesterov, axis=(-3, -1), keepdims=True)) + norm_epsilon
    iterate = nesterov / frobenius
    for step in range(ITERS):
        gram_matrix = jnp.einsum(
            "...rhc,...rhd->...hcd", iterate, iterate, precision=lax.Precision.HIGHEST
        )
        poly_matrix = quintic_second * gram_matrix + quintic_third * jnp.einsum(
            "...hcd,...hde->...hce", gram_matrix, gram_matrix, precision=lax.Precision.HIGHEST
        )
        iterate = quintic_first * iterate + jnp.einsum(
            "...rhc,...hcd->...rhd", iterate, poly_matrix, precision=lax.Precision.HIGHEST
        )
    return iterate


def shards(features, cotangents, labels, diff_mask, class_weight, owners, momentum):
    dp_count = lax.axis_size("dp")
    tensor_count = lax.axis_size("tensor")
    local_tokens = cotangents.shape[0]
    scaled = weigh(cotangents, labels, diff_mask, class_weight, local_tokens * dp_count)
    heads_here = owners.shape[0]
    head_width = cotangents.shape[1] // heads_here
    block_rows = features.shape[0] * tensor_count // dp_count
    inverse = invert(owners)
    all_heads = lax.all_gather(scaled, "tensor", axis=1, tiled=True)
    rows_all_heads = jnp.dot(features, all_heads, preferred_element_type=jnp.float32)
    partial_grad = lax.all_to_all(
        rows_all_heads.reshape(features.shape[0], tensor_count, head_width),
        "tensor",
        split_axis=1,
        concat_axis=0,
        tiled=True,
    ).reshape(features.shape[0] * tensor_count, head_width)
    blocks = partial_grad.reshape(dp_count, block_rows, heads_here * head_width)
    in_owner_order = jnp.take(blocks, inverse[0], axis=0).reshape(dp_count * block_rows, heads_here * head_width)
    own_block = lax.psum_scatter(in_owner_order, "dp", scatter_dimension=0, tiled=True).reshape(
        block_rows, heads_here, head_width
    )
    previous = momentum.reshape(block_rows, heads_here, head_width)
    new_momentum = decay_rate * previous + own_block
    nesterov = own_block + decay_rate * new_momentum
    ortho = orthogonalize(nesterov)
    own_update = (
        (ortho * math.sqrt(block_rows))
        .astype(jnp.bfloat16)
        .reshape(block_rows, heads_here * head_width)
    )
    gathered = lax.all_gather(own_update, "dp", axis=0, tiled=True)
    placed = reorder(gathered.reshape(dp_count, block_rows, heads_here, head_width), owners)
    return (
        placed.reshape(dp_count * block_rows, heads_here * head_width),
        new_momentum.reshape(block_rows, heads_here * head_width),
    )


def solution(mesh):
    in_specs = (
        P("tensor", "dp"),
        P("dp", "tensor"),
        P("dp"),
        P("dp"),
        P(),
        P("tensor", None),
        P("dp", "tensor"),
    )
    out_specs = (P(None, "tensor"), P("dp", "tensor"))
    return jax.shard_map(shards, mesh=mesh, in_specs=in_specs, out_specs=out_specs, check_vma=False)
```

```python
import math

import jax
import numpy as np
import jax.numpy as jnp
from jax import lax
from jax.sharding import Mesh, PartitionSpec as P

ITERS = 5


decay_rate = 0.95
quintic_first = 3.4445
quintic_second = -4.775
quintic_third = 2.0315
norm_epsilon = 1e-07


def weigh(cotangents, labels, diff_mask, class_weight, total_tokens):
    classes = jnp.arange(class_weight.shape[0], dtype=jnp.int32)
    picked = (labels[:, None] == classes[None, :]).astype(jnp.float32)
    token_weight = diff_mask.astype(jnp.float32) * jnp.sum(picked * class_weight[None, :], axis=1)
    factor = token_weight / math.sqrt(total_tokens)
    return (cotangents.astype(jnp.float32) * factor[:, None]).astype(jnp.bfloat16)


def invert(owners):
    number = owners.shape[1]
    candidates = jnp.arange(number, dtype=jnp.int32)
    matches = owners[:, None, :] == candidates[None, :, None]
    return jnp.sum(jnp.where(matches, candidates[None, None, :], 0), axis=2)


def reorder(blocks, lookup):
    return jnp.take_along_axis(blocks, jnp.transpose(lookup)[:, None, :, None], axis=0)


def orthogonalize(nesterov):
    frobenius = jnp.sqrt(jnp.sum(nesterov * nesterov, axis=(-3, -1), keepdims=True)) + norm_epsilon
    iterate = nesterov / frobenius
    for step in range(ITERS):
        gram_matrix = jnp.einsum(
            "...rhc,...rhd->...hcd", iterate, iterate, precision=lax.Precision.HIGHEST
        )
        poly_matrix = quintic_second * gram_matrix + quintic_third * jnp.einsum(
            "...hcd,...hde->...hce", gram_matrix, gram_matrix, precision=lax.Precision.HIGHEST
        )
        iterate = quintic_first * iterate + jnp.einsum(
            "...rhc,...hcd->...rhd", iterate, poly_matrix, precision=lax.Precision.HIGHEST
        )
    return iterate


def staged_sum_scatter(blocks, axes):
    for axis in axes:
        blocks = lax.psum_scatter(blocks, axis, scatter_dimension=0, tiled=True)
    return blocks


def staged_gather(piece, axes):
    for axis in axes:
        piece = lax.all_gather(piece, axis, axis=0, tiled=True)
    return piece


def scatter_position(sizes, order):
    count = int(np.prod(sizes))
    coords = np.stack(np.unravel_index(np.arange(count), sizes), axis=1)
    position = np.zeros(count, dtype=np.int64)
    for axis in order:
        position = position * sizes[axis] + coords[:, axis]
    return position


def shards(features, cotangents, labels, diff_mask, class_weight, owners, momentum):
    dp_count = lax.axis_size(DP)
    tensor_count = lax.axis_size(TP)
    local_tokens = cotangents.shape[0]
    scaled = weigh(cotangents, labels, diff_mask, class_weight, local_tokens * dp_count)
    heads_here = owners.shape[0]
    head_width = cotangents.shape[1] // heads_here
    block_rows = features.shape[0] * tensor_count // dp_count
    inverse = invert(owners)
    dp_sizes = tuple(lax.axis_size(axis) for axis in DP)
    partial_grad = jnp.dot(
        staged_gather(features, ("xh", "y")),
        scaled,
        preferred_element_type=jnp.float32,
    )
    blocks = partial_grad.reshape(dp_count, block_rows, heads_here * head_width)
    position = scatter_position(dp_sizes, (2, 1, 0))
    owner_at = np.argsort(position)
    in_owner_order = jnp.take(blocks, inverse[0][owner_at], axis=0).reshape(
        dp_count * block_rows, heads_here * head_width
    )
    own_block = staged_sum_scatter(in_owner_order, ("c", "xl", "z")).reshape(
        block_rows, heads_here, head_width
    )
    previous = momentum.reshape(block_rows, heads_here, head_width)
    new_momentum = decay_rate * previous + own_block
    nesterov = own_block + decay_rate * new_momentum
    ortho = orthogonalize(nesterov)
    own_update = (
        (ortho * math.sqrt(block_rows))
        .astype(jnp.bfloat16)
        .reshape(block_rows, heads_here * head_width)
    )
    gathered = staged_gather(own_update, ("z", "xl", "c"))
    gather_at = jnp.asarray(scatter_position(dp_sizes, (2, 1, 0)), dtype=jnp.int32)
    placed = reorder(
        gathered.reshape(dp_count, block_rows, heads_here, head_width), gather_at[owners]
    )
    return (
        placed.reshape(dp_count * block_rows, heads_here * head_width),
        new_momentum.reshape(block_rows, heads_here * head_width),
    )


DP = ("z", "xl", "c")
TP = ("y", "xh")


def solution(mesh):
    dp_size, tp_size = mesh.shape["dp"], mesh.shape["tensor"]
    fine = Mesh(
        mesh.devices.reshape(dp_size // 4, 2, 2, tp_size // 2, 2),
        DP + TP,
    )
    in_specs = (
        P(TP, DP),
        P(DP, TP),
        P(DP),
        P(DP),
        P(),
        P(TP, None),
        P(DP, TP),
    )
    out_specs = (P(None, TP), P(DP, TP))
    return jax.shard_map(shards, mesh=fine, in_specs=in_specs, out_specs=out_specs, check_vma=False)
```

```python
import math

import jax
import jax.numpy as jnp
from jax import lax
from jax.sharding import Mesh, PartitionSpec as P

ITERS = 5


decay_rate = 0.95
quintic_first = 3.4445
quintic_second = -4.775
quintic_third = 2.0315
norm_epsilon = 1e-07

DP = ("z", "xl", "c")
TP = ("y", "xh")
SWAP = [(0, 1), (1, 0)]


def weigh(cotangents, labels, diff_mask, class_weight, total_tokens):
    classes = jnp.arange(class_weight.shape[0], dtype=jnp.int32)
    picked = (labels[:, None] == classes[None, :]).astype(jnp.float32)
    token_weight = diff_mask.astype(jnp.float32) * jnp.sum(picked * class_weight[None, :], axis=1)
    factor = token_weight / math.sqrt(total_tokens)
    return (cotangents.astype(jnp.float32) * factor[:, None]).astype(jnp.bfloat16)


def invert(owners):
    number = owners.shape[1]
    candidates = jnp.arange(number, dtype=jnp.int32)
    matches = owners[:, None, :] == candidates[None, :, None]
    return jnp.sum(jnp.where(matches, candidates[None, None, :], 0), axis=2)


def reorder(blocks, lookup):
    return jnp.take_along_axis(blocks, jnp.transpose(lookup)[:, None, :, None], axis=0)


def orthogonalize(nesterov):
    frobenius = jnp.sqrt(jnp.sum(nesterov * nesterov, axis=(-3, -1), keepdims=True)) + norm_epsilon
    iterate = nesterov / frobenius
    for step in range(ITERS):
        gram_matrix = jnp.einsum(
            "...rhc,...rhd->...hcd", iterate, iterate, precision=lax.Precision.HIGHEST
        )
        poly_matrix = quintic_second * gram_matrix + quintic_third * jnp.einsum(
            "...hcd,...hde->...hce", gram_matrix, gram_matrix, precision=lax.Precision.HIGHEST
        )
        iterate = quintic_first * iterate + jnp.einsum(
            "...rhc,...hcd->...rhd", iterate, poly_matrix, precision=lax.Precision.HIGHEST
        )
    return iterate


def pair_sum_scatter(blocks, axis):
    half = blocks.shape[0] // 2
    return blocks[:half] + lax.ppermute(blocks[half:], axis, SWAP)


def pair_gather(piece, axis):
    return jnp.concatenate([piece, lax.ppermute(piece, axis, SWAP)], axis=0)


def shards(features, cotangents, labels, diff_mask, class_weight, owners, momentum):
    dp_count = lax.axis_size(DP)
    z_count = lax.axis_size("z")
    tensor_count = lax.axis_size(TP)
    local_tokens = cotangents.shape[0]
    scaled = weigh(cotangents, labels, diff_mask, class_weight, local_tokens * dp_count)
    heads_here = owners.shape[0]
    head_width = cotangents.shape[1] // heads_here
    feature_rows = features.shape[0]
    block_rows = feature_rows * tensor_count // dp_count
    sub_blocks = feature_rows // block_rows
    inverse = invert(owners)
    z = lax.axis_index("z")
    xl = lax.axis_index("xl")
    c = lax.axis_index("c")
    xh = lax.axis_index("xh")

    pair_rows = pair_gather(features, "xh")
    all_rows = lax.all_gather(pair_rows, "y", axis=0, tiled=True)
    partial_grad = jnp.dot(all_rows, scaled, preferred_element_type=jnp.float32)
    k = sub_blocks
    b = jnp.arange(dp_count, dtype=jnp.int32)
    pair_slot = jnp.where((b // k) % 2 == xh, 0, 1)
    block_position = (b // (2 * k)) * (2 * k) + pair_slot * k + b % k

    p = jnp.arange(dp_count, dtype=jnp.int32)
    half, quarter = dp_count // 2, dp_count // 4
    owner_c = jnp.where(p < half, c, 1 - c)
    owner_xl = jnp.where(p % half < quarter, xl, 1 - xl)
    owner_z = p % quarter
    owner = owner_z * 4 + owner_xl * 2 + owner_c
    blocks = partial_grad.reshape(dp_count, block_rows, heads_here * head_width)
    in_scatter_order = jnp.take(blocks, block_position[inverse[0][owner]], axis=0)
    kept = pair_sum_scatter(in_scatter_order, "c")
    kept = pair_sum_scatter(kept, "xl")
    own_block = lax.psum_scatter(
        kept.reshape(z_count * block_rows, heads_here * head_width), "z", scatter_dimension=0, tiled=True
    ).reshape(block_rows, heads_here, head_width)

    previous = momentum.reshape(block_rows, heads_here, head_width)
    new_momentum = decay_rate * previous + own_block
    nesterov = own_block + decay_rate * new_momentum
    ortho = orthogonalize(nesterov)
    own_update = (
        (ortho * math.sqrt(block_rows))
        .astype(jnp.bfloat16)
        .reshape(block_rows, heads_here * head_width)
    )
    gathered = lax.all_gather(own_update, "z", axis=0, tiled=True)
    gathered = pair_gather(gathered, "xl")
    gathered = pair_gather(gathered, "c")
    d = jnp.arange(dp_count, dtype=jnp.int32)
    update_position = (
        jnp.where(d % 2 == c, 0, half) + jnp.where((d // 2) % 2 == xl, 0, quarter) + d // 4
    )
    placed = reorder(
        gathered.reshape(dp_count, block_rows, heads_here, head_width), update_position[owners]
    )
    return (
        placed.reshape(dp_count * block_rows, heads_here * head_width),
        new_momentum.reshape(block_rows, heads_here * head_width),
    )


def solution(mesh):
    dp_size, tp_size = mesh.shape["dp"], mesh.shape["tensor"]
    fine = Mesh(mesh.devices.reshape(dp_size // 4, 2, 2, tp_size // 2, 2), DP + TP)
    in_specs = (
        P(TP, DP),
        P(DP, TP),
        P(DP),
        P(DP),
        P(),
        P(TP, None),
        P(DP, TP),
    )
    out_specs = (P(None, TP), P(DP, TP))
    return jax.shard_map(shards, mesh=fine, in_specs=in_specs, out_specs=out_specs, check_vma=False)
```

```python
import math

import jax
import jax.numpy as jnp
from jax import lax
from jax.sharding import Mesh, PartitionSpec as P

ITERS = 5


decay_rate = 0.95
quintic_first = 3.4445
quintic_second = -4.775
quintic_third = 2.0315
norm_epsilon = 1e-07

DP = ("z", "xl", "c")
TP = ("y", "xh")
SWAP = [(0, 1), (1, 0)]


def weigh(cotangents, labels, diff_mask, class_weight, total_tokens):
    classes = jnp.arange(class_weight.shape[0], dtype=jnp.int32)
    picked = (labels[:, None] == classes[None, :]).astype(jnp.float32)
    token_weight = diff_mask.astype(jnp.float32) * jnp.sum(picked * class_weight[None, :], axis=1)
    factor = token_weight / math.sqrt(total_tokens)
    return (cotangents.astype(jnp.float32) * factor[:, None]).astype(jnp.bfloat16)


def invert(owners):
    number = owners.shape[1]
    candidates = jnp.arange(number, dtype=jnp.int32)
    matches = owners[:, None, :] == candidates[None, :, None]
    return jnp.sum(jnp.where(matches, candidates[None, None, :], 0), axis=2)


def reorder(blocks, lookup):
    return jnp.take_along_axis(blocks, jnp.transpose(lookup)[:, None, :, None], axis=0)


def orthogonalize(nesterov):
    frobenius = jnp.sqrt(jnp.sum(nesterov * nesterov, axis=(-3, -1), keepdims=True)) + norm_epsilon
    iterate = nesterov / frobenius
    for step in range(ITERS):
        gram_matrix = jnp.einsum(
            "...rhc,...rhd->...hcd", iterate, iterate, precision=lax.Precision.HIGHEST
        )
        poly_matrix = quintic_second * gram_matrix + quintic_third * jnp.einsum(
            "...hcd,...hde->...hce", gram_matrix, gram_matrix, precision=lax.Precision.HIGHEST
        )
        iterate = quintic_first * iterate + jnp.einsum(
            "...rhc,...hcd->...rhd", iterate, poly_matrix, precision=lax.Precision.HIGHEST
        )
    return iterate


def pair_sum_scatter(blocks, axis):
    half = blocks.shape[0] // 2
    return blocks[:half] + lax.ppermute(blocks[half:], axis, SWAP)


def pair_gather(piece, axis):
    return jnp.concatenate([piece, lax.ppermute(piece, axis, SWAP)], axis=0)


def shards(features, cotangents, labels, diff_mask, class_weight, owners, momentum):
    dp_count = lax.axis_size(DP)
    z_count = lax.axis_size("z")
    tensor_count = lax.axis_size(TP)
    local_tokens = cotangents.shape[0]
    scaled = weigh(cotangents, labels, diff_mask, class_weight, local_tokens * dp_count)
    heads_here = owners.shape[0]
    head_width = cotangents.shape[1] // heads_here
    feature_rows = features.shape[0]
    block_rows = feature_rows * tensor_count // dp_count
    sub_blocks = feature_rows // block_rows
    inverse = invert(owners)
    z = lax.axis_index("z")
    xl = lax.axis_index("xl")
    c = lax.axis_index("c")
    xh = lax.axis_index("xh")

    y_count = lax.axis_size("y")
    half, quarter = dp_count // 2, dp_count // 4
    quarter_rows = block_rows // 4
    pair_rows = pair_gather(features, "xh")
    heads_y = lax.all_gather(scaled, "y", axis=1, tiled=True)
    pair_blocks = 2 * sub_blocks
    group_rows = pair_blocks * quarter_rows
    position = jnp.arange(2 * feature_rows, dtype=jnp.int32)
    group = position // group_rows
    within = position % group_rows
    j = within // quarter_rows
    r = within % quarter_rows
    quarter_xl = jnp.where(group % 2 == 0, xl, 1 - xl)
    quarter_c = jnp.where(group < 2, c, 1 - c)
    u = 2 * quarter_xl + quarter_c
    shard_slot = jnp.where(j // sub_blocks == xh, 0, 1)
    source_row = shard_slot * feature_rows + (j % sub_blocks) * block_rows + u * quarter_rows + r
    arranged = jnp.take(pair_rows, source_row, axis=0)
    partial = jnp.dot(arranged, heads_y, preferred_element_type=jnp.float32).reshape(
        2 * feature_rows, y_count, head_width
    )
    kept = pair_sum_scatter(partial, "c")
    kept = pair_sum_scatter(kept, "xl")
    quarters = lax.all_to_all(kept, "y", split_axis=1, concat_axis=0, tiled=True).reshape(
        dp_count, quarter_rows, head_width
    )
    in_owner_order = jnp.take(quarters, inverse[0], axis=0).reshape(
        dp_count * quarter_rows, head_width
    )
    local_owners = lax.psum_scatter(in_owner_order, "z", scatter_dimension=0, tiled=True)
    own_block = lax.all_to_all(
        local_owners, ("xl", "c"), split_axis=0, concat_axis=0, tiled=True
    ).reshape(block_rows, heads_here, head_width)

    previous = momentum.reshape(block_rows, heads_here, head_width)
    new_momentum = decay_rate * previous + own_block
    nesterov = own_block + decay_rate * new_momentum
    ortho = orthogonalize(nesterov)
    own_update = (
        (ortho * math.sqrt(block_rows))
        .astype(jnp.bfloat16)
        .reshape(block_rows, heads_here * head_width)
    )
    gathered = lax.all_gather(own_update, "z", axis=0, tiled=True)
    gathered = pair_gather(gathered, "xl")
    gathered = pair_gather(gathered, "c")
    d = jnp.arange(dp_count, dtype=jnp.int32)
    update_position = (
        jnp.where(d % 2 == c, 0, half) + jnp.where((d // 2) % 2 == xl, 0, quarter) + d // 4
    )
    placed = reorder(
        gathered.reshape(dp_count, block_rows, heads_here, head_width), update_position[owners]
    )
    return (
        placed.reshape(dp_count * block_rows, heads_here * head_width),
        new_momentum.reshape(block_rows, heads_here * head_width),
    )


def solution(mesh):
    dp_size, tp_size = mesh.shape["dp"], mesh.shape["tensor"]
    fine = Mesh(mesh.devices.reshape(dp_size // 4, 2, 2, tp_size // 2, 2), DP + TP)
    in_specs = (
        P(TP, DP),
        P(DP, TP),
        P(DP),
        P(DP),
        P(),
        P(TP, None),
        P(DP, TP),
    )
    out_specs = (P(None, TP), P(DP, TP))
    return jax.shard_map(shards, mesh=fine, in_specs=in_specs, out_specs=out_specs, check_vma=False)
```

```python
import math

import jax
import jax.numpy as jnp
from jax import lax
from jax.sharding import Mesh, PartitionSpec as P

ITERS = 5


decay_rate = 0.95
quintic_first = 3.4445
quintic_second = -4.775
quintic_third = 2.0315
norm_epsilon = 1e-07

DP = ("z", "xl", "c")
TP = ("y", "xh")
SWAP = [(0, 1), (1, 0)]


def weigh(cotangents, labels, diff_mask, class_weight, total_tokens):
    classes = jnp.arange(class_weight.shape[0], dtype=jnp.int32)
    picked = (labels[:, None] == classes[None, :]).astype(jnp.float32)
    token_weight = diff_mask.astype(jnp.float32) * jnp.sum(picked * class_weight[None, :], axis=1)
    factor = token_weight / math.sqrt(total_tokens)
    return (cotangents.astype(jnp.float32) * factor[:, None]).astype(jnp.bfloat16)


def invert(owners):
    number = owners.shape[1]
    candidates = jnp.arange(number, dtype=jnp.int32)
    matches = owners[:, None, :] == candidates[None, :, None]
    return jnp.sum(jnp.where(matches, candidates[None, None, :], 0), axis=2)


def reorder(blocks, lookup):
    return jnp.take_along_axis(blocks, jnp.transpose(lookup)[:, None, :, None], axis=0)


def orthogonalize(nesterov):
    frobenius = jnp.sqrt(jnp.sum(nesterov * nesterov, axis=(-3, -1), keepdims=True)) + norm_epsilon
    iterate = nesterov / frobenius
    for step in range(ITERS):
        gram_matrix = jnp.einsum(
            "...rhc,...rhd->...hcd", iterate, iterate, precision=lax.Precision.HIGHEST
        )
        poly_matrix = quintic_second * gram_matrix + quintic_third * jnp.einsum(
            "...hcd,...hde->...hce", gram_matrix, gram_matrix, precision=lax.Precision.HIGHEST
        )
        iterate = quintic_first * iterate + jnp.einsum(
            "...rhc,...hcd->...rhd", iterate, poly_matrix, precision=lax.Precision.HIGHEST
        )
    return iterate


def pair_sum_scatter(blocks, axis):
    half = blocks.shape[0] // 2
    return blocks[:half] + lax.ppermute(blocks[half:], axis, SWAP)


def xor_sum_scatter(blocks, axis, distance):
    half = blocks.shape[0] // 2
    count = lax.axis_size(axis)
    perm = [(i, i ^ distance) for i in range(count)]
    return blocks[:half] + lax.ppermute(blocks[half:], axis, perm)


def xor_gather(piece, axis, distance):
    count = lax.axis_size(axis)
    perm = [(i, i ^ distance) for i in range(count)]
    return jnp.concatenate([piece, lax.ppermute(piece, axis, perm)], axis=0)


def ring_gather(piece, axis):
    count = lax.axis_size(axis)
    to_right = [(i, (i + 1) % count) for i in range(count)]
    to_left = [(i, (i - 1) % count) for i in range(count)]
    pieces = [piece]
    from_left = from_right = piece
    for step in range(1, count // 2 + 1):
        from_left = lax.ppermute(from_left, axis, to_right)
        pieces.append(from_left)
        if 2 * step < count:
            from_right = lax.ppermute(from_right, axis, to_left)
            pieces.append(from_right)
    return jnp.stack(pieces)


def pair_gather(piece, axis):
    return jnp.concatenate([piece, lax.ppermute(piece, axis, SWAP)], axis=0)


def shards(features, cotangents, labels, diff_mask, class_weight, owners, momentum):
    dp_count = lax.axis_size(DP)
    z_count = lax.axis_size("z")
    tensor_count = lax.axis_size(TP)
    local_tokens = cotangents.shape[0]
    scaled = weigh(cotangents, labels, diff_mask, class_weight, local_tokens * dp_count)
    heads_here = owners.shape[0]
    head_width = cotangents.shape[1] // heads_here
    feature_rows = features.shape[0]
    block_rows = feature_rows * tensor_count // dp_count
    sub_blocks = feature_rows // block_rows
    inverse = invert(owners)
    z = lax.axis_index("z")
    xl = lax.axis_index("xl")
    c = lax.axis_index("c")
    xh = lax.axis_index("xh")

    y_count = lax.axis_size("y")
    half, quarter = dp_count // 2, dp_count // 4
    quarter_rows = block_rows // 4
    pair_rows = pair_gather(features, "xh")
    y = lax.axis_index("y")
    ring_pieces = ring_gather(scaled, "y")
    head = jnp.arange(y_count, dtype=jnp.int32)
    ahead = (head - y) % y_count
    behind = (y - head) % y_count
    slot = jnp.where(ahead == 0, 0, jnp.where(ahead < behind, 2 * ahead, 2 * behind - 1))
    heads_y = jnp.transpose(jnp.take(ring_pieces, slot, axis=0), (1, 0, 2)).reshape(
        local_tokens, y_count * head_width
    )
    pair_blocks = 2 * sub_blocks
    group_rows = pair_blocks * quarter_rows
    position = jnp.arange(2 * feature_rows, dtype=jnp.int32)
    group = position // group_rows
    within = position % group_rows
    j = within // quarter_rows
    r = within % quarter_rows
    quarter_xl = jnp.where(group % 2 == 0, xl, 1 - xl)
    quarter_c = jnp.where(group < 2, c, 1 - c)
    u = 2 * quarter_xl + quarter_c
    shard_slot = jnp.where(j // sub_blocks == xh, 0, 1)
    source_row = shard_slot * feature_rows + (j % sub_blocks) * block_rows + u * quarter_rows + r
    arranged = jnp.take(pair_rows, source_row, axis=0)
    partial = jnp.dot(arranged, heads_y, preferred_element_type=jnp.float32).reshape(
        2 * feature_rows, y_count, head_width
    )
    kept = pair_sum_scatter(partial, "c")
    kept = pair_sum_scatter(kept, "xl")
    quarters = lax.all_to_all(kept, "y", split_axis=1, concat_axis=0, tiled=True).reshape(
        dp_count, quarter_rows, head_width
    )
    p = jnp.arange(dp_count, dtype=jnp.int32)
    per_z = dp_count // z_count
    flips = (p // half) % 2 + 2 * ((p // quarter) % 2) + 4 * ((p // (quarter // 2)) % 2)
    owner = per_z * (z ^ flips) + p % per_z
    in_owner_order = jnp.take(quarters, inverse[0][owner], axis=0)
    kept = in_owner_order
    for distance in (1, 2, 4):
        kept = xor_sum_scatter(kept, "z", distance)
    local_owners = kept.reshape(per_z * quarter_rows, head_width)
    own_block = lax.all_to_all(
        local_owners, ("xl", "c"), split_axis=0, concat_axis=0, tiled=True
    ).reshape(block_rows, heads_here, head_width)

    previous = momentum.reshape(block_rows, heads_here, head_width)
    new_momentum = decay_rate * previous + own_block
    nesterov = own_block + decay_rate * new_momentum
    ortho = orthogonalize(nesterov)
    own_update = (
        (ortho * math.sqrt(block_rows))
        .astype(jnp.bfloat16)
        .reshape(block_rows, heads_here * head_width)
    )
    gathered = own_update
    for distance in (1, 2, 4):
        gathered = xor_gather(gathered, "z", distance)
    gathered = pair_gather(gathered, "xl")
    gathered = pair_gather(gathered, "c")
    d = jnp.arange(dp_count, dtype=jnp.int32)
    update_position = (
        jnp.where(d % 2 == c, 0, half) + jnp.where((d // 2) % 2 == xl, 0, quarter) + ((d // 4) ^ z)
    )
    placed = reorder(
        gathered.reshape(dp_count, block_rows, heads_here, head_width), update_position[owners]
    )
    return (
        placed.reshape(dp_count * block_rows, heads_here * head_width),
        new_momentum.reshape(block_rows, heads_here * head_width),
    )


def solution(mesh):
    dp_size, tp_size = mesh.shape["dp"], mesh.shape["tensor"]
    fine = Mesh(mesh.devices.reshape(dp_size // 4, 2, 2, tp_size // 2, 2), DP + TP)
    in_specs = (
        P(TP, DP),
        P(DP, TP),
        P(DP),
        P(DP),
        P(),
        P(TP, None),
        P(DP, TP),
    )
    out_specs = (P(None, TP), P(DP, TP))
    return jax.shard_map(shards, mesh=fine, in_specs=in_specs, out_specs=out_specs, check_vma=False)
```

```python
import math

import jax
import jax.numpy as jnp
from jax import lax
from jax.sharding import Mesh, PartitionSpec as P

ITERS = 5


decay_rate = 0.95
quintic_first = 3.4445
quintic_second = -4.775
quintic_third = 2.0315
norm_epsilon = 1e-07

DP = ("z", "xl", "c")
TP = ("y", "xh")
SWAP = [(0, 1), (1, 0)]


def weigh(cotangents, labels, diff_mask, class_weight, total_tokens):
    classes = jnp.arange(class_weight.shape[0], dtype=jnp.int32)
    picked = (labels[:, None] == classes[None, :]).astype(jnp.float32)
    token_weight = diff_mask.astype(jnp.float32) * jnp.sum(picked * class_weight[None, :], axis=1)
    factor = token_weight / math.sqrt(total_tokens)
    return (cotangents.astype(jnp.float32) * factor[:, None]).astype(jnp.bfloat16)


def invert(owners):
    number = owners.shape[1]
    candidates = jnp.arange(number, dtype=jnp.int32)
    matches = owners[:, None, :] == candidates[None, :, None]
    return jnp.sum(jnp.where(matches, candidates[None, None, :], 0), axis=2)


def reorder(blocks, lookup):
    return jnp.take_along_axis(blocks, jnp.transpose(lookup)[:, None, :, None], axis=0)


def orthogonalize(nesterov):
    frobenius = jnp.sqrt(jnp.sum(nesterov * nesterov, axis=(-3, -1), keepdims=True)) + norm_epsilon
    iterate = nesterov / frobenius
    for step in range(ITERS):
        gram_matrix = jnp.einsum(
            "...rhc,...rhd->...hcd", iterate, iterate, precision=lax.Precision.HIGHEST
        )
        poly_matrix = quintic_second * gram_matrix + quintic_third * jnp.einsum(
            "...hcd,...hde->...hce", gram_matrix, gram_matrix, precision=lax.Precision.HIGHEST
        )
        iterate = quintic_first * iterate + jnp.einsum(
            "...rhc,...hcd->...rhd", iterate, poly_matrix, precision=lax.Precision.HIGHEST
        )
    return iterate


def pair_sum_scatter(blocks, axis):
    half = blocks.shape[0] // 2
    return blocks[:half] + lax.ppermute(blocks[half:], axis, SWAP)


def xor_sum_scatter(blocks, axis, distance):
    half = blocks.shape[0] // 2
    count = lax.axis_size(axis)
    perm = [(i, i ^ distance) for i in range(count)]
    return blocks[:half] + lax.ppermute(blocks[half:], axis, perm)


def xor_gather(piece, axis, distance):
    count = lax.axis_size(axis)
    perm = [(i, i ^ distance) for i in range(count)]
    return jnp.concatenate([piece, lax.ppermute(piece, axis, perm)], axis=0)


def ring_gather(piece, axis):
    count = lax.axis_size(axis)
    to_right = [(i, (i + 1) % count) for i in range(count)]
    to_left = [(i, (i - 1) % count) for i in range(count)]
    pieces = [piece]
    from_left = from_right = piece
    for step in range(1, count // 2 + 1):
        from_left = lax.ppermute(from_left, axis, to_right)
        pieces.append(from_left)
        if 2 * step < count:
            from_right = lax.ppermute(from_right, axis, to_left)
            pieces.append(from_right)
    return jnp.stack(pieces)


def pair_gather(piece, axis):
    return jnp.concatenate([piece, lax.ppermute(piece, axis, SWAP)], axis=0)


def shards(features, cotangents, labels, diff_mask, class_weight, owners, momentum):
    dp_count = lax.axis_size(DP)
    z_count = lax.axis_size("z")
    tensor_count = lax.axis_size(TP)
    local_tokens = cotangents.shape[0]
    scaled = weigh(cotangents, labels, diff_mask, class_weight, local_tokens * dp_count)
    heads_here = owners.shape[0]
    head_width = cotangents.shape[1] // heads_here
    feature_rows = features.shape[0]
    block_rows = feature_rows * tensor_count // dp_count
    sub_blocks = feature_rows // block_rows
    inverse = invert(owners)
    z = lax.axis_index("z")
    xl = lax.axis_index("xl")
    c = lax.axis_index("c")
    xh = lax.axis_index("xh")

    y_count = lax.axis_size("y")
    half, quarter = dp_count // 2, dp_count // 4
    quarter_rows = block_rows // 4
    pair_rows = pair_gather(features, "xh")
    y = lax.axis_index("y")
    ring_pieces = ring_gather(scaled, "y")
    head = jnp.arange(y_count, dtype=jnp.int32)
    ahead = (head - y) % y_count
    behind = (y - head) % y_count
    slot = jnp.where(ahead == 0, 0, jnp.where(ahead < behind, 2 * ahead, 2 * behind - 1))
    heads_y = jnp.transpose(jnp.take(ring_pieces, slot, axis=0), (1, 0, 2)).reshape(
        local_tokens, y_count * head_width
    )
    pair_blocks = 2 * sub_blocks
    group_rows = pair_blocks * quarter_rows
    position = jnp.arange(2 * feature_rows, dtype=jnp.int32)
    group = position // group_rows
    within = position % group_rows
    j = within // quarter_rows
    r = within % quarter_rows
    quarter_xl = jnp.where(group % 2 == 0, xl, 1 - xl)
    quarter_c = jnp.where(group < 2, c, 1 - c)
    u = 2 * quarter_xl + quarter_c
    shard_slot = jnp.where(j // sub_blocks == xh, 0, 1)
    source_row = shard_slot * feature_rows + (j % sub_blocks) * block_rows + u * quarter_rows + r
    arranged = jnp.take(pair_rows, source_row, axis=0)
    partial = jnp.dot(arranged, heads_y, preferred_element_type=jnp.float32).reshape(
        2 * feature_rows, y_count, head_width
    )
    kept = pair_sum_scatter(partial, "c")
    kept = pair_sum_scatter(kept, "xl")
    quarters = lax.all_to_all(kept, "y", split_axis=1, concat_axis=0, tiled=True).reshape(
        dp_count, quarter_rows, head_width
    )
    in_owner_order = jnp.take(quarters, inverse[0], axis=0)
    from_all = lax.all_to_all(in_owner_order, DP, split_axis=0, concat_axis=0, tiled=True)
    own_block = jnp.sum(
        from_all.reshape(z_count, dp_count // z_count, quarter_rows, head_width), axis=0
    ).reshape(block_rows, heads_here, head_width)

    previous = momentum.reshape(block_rows, heads_here, head_width)
    new_momentum = decay_rate * previous + own_block
    nesterov = own_block + decay_rate * new_momentum
    ortho = orthogonalize(nesterov)
    own_update = (
        (ortho * math.sqrt(block_rows))
        .astype(jnp.bfloat16)
        .reshape(block_rows, heads_here * head_width)
    )
    gathered = lax.all_to_all(
        jnp.broadcast_to(own_update[None], (dp_count,) + own_update.shape),
        DP,
        split_axis=0,
        concat_axis=0,
        tiled=True,
    )
    placed = reorder(gathered.reshape(dp_count, block_rows, heads_here, head_width), owners)
    return (
        placed.reshape(dp_count * block_rows, heads_here * head_width),
        new_momentum.reshape(block_rows, heads_here * head_width),
    )


def solution(mesh):
    dp_size, tp_size = mesh.shape["dp"], mesh.shape["tensor"]
    fine = Mesh(mesh.devices.reshape(dp_size // 4, 2, 2, tp_size // 2, 2), DP + TP)
    in_specs = (
        P(TP, DP),
        P(DP, TP),
        P(DP),
        P(DP),
        P(),
        P(TP, None),
        P(DP, TP),
    )
    out_specs = (P(None, TP), P(DP, TP))
    return jax.shard_map(shards, mesh=fine, in_specs=in_specs, out_specs=out_specs, check_vma=False)
```

```python
import math

import jax
import jax.numpy as jnp
from jax import lax
from jax.sharding import Mesh, PartitionSpec as P

ITERS = 5


decay_rate = 0.95
quintic_first = 3.4445
quintic_second = -4.775
quintic_third = 2.0315
norm_epsilon = 1e-07

DP = ("z", "xl", "c")
TP = ("y", "xh")
SWAP = [(0, 1), (1, 0)]


def weigh(cotangents, labels, diff_mask, class_weight, total_tokens):
    classes = jnp.arange(class_weight.shape[0], dtype=jnp.int32)
    picked = (labels[:, None] == classes[None, :]).astype(jnp.float32)
    token_weight = diff_mask.astype(jnp.float32) * jnp.sum(picked * class_weight[None, :], axis=1)
    factor = token_weight / math.sqrt(total_tokens)
    return (cotangents.astype(jnp.float32) * factor[:, None]).astype(jnp.bfloat16)


def invert(owners):
    number = owners.shape[1]
    candidates = jnp.arange(number, dtype=jnp.int32)
    matches = owners[:, None, :] == candidates[None, :, None]
    return jnp.sum(jnp.where(matches, candidates[None, None, :], 0), axis=2)


def reorder(blocks, lookup):
    return jnp.take_along_axis(blocks, jnp.transpose(lookup)[:, None, :, None], axis=0)


def orthogonalize(nesterov):
    frobenius = jnp.sqrt(jnp.sum(nesterov * nesterov, axis=(-3, -1), keepdims=True)) + norm_epsilon
    iterate = nesterov / frobenius
    for step in range(ITERS):
        gram_matrix = jnp.einsum(
            "...rhc,...rhd->...hcd", iterate, iterate, precision=lax.Precision.HIGHEST
        )
        poly_matrix = quintic_second * gram_matrix + quintic_third * jnp.einsum(
            "...hcd,...hde->...hce", gram_matrix, gram_matrix, precision=lax.Precision.HIGHEST
        )
        iterate = quintic_first * iterate + jnp.einsum(
            "...rhc,...hcd->...rhd", iterate, poly_matrix, precision=lax.Precision.HIGHEST
        )
    return iterate


def pair_sum_scatter(blocks, axis):
    half = blocks.shape[0] // 2
    return blocks[:half] + lax.ppermute(blocks[half:], axis, SWAP)


def xor_sum_scatter(blocks, axis, distance):
    half = blocks.shape[0] // 2
    count = lax.axis_size(axis)
    perm = [(i, i ^ distance) for i in range(count)]
    return blocks[:half] + lax.ppermute(blocks[half:], axis, perm)


def xor_gather(piece, axis, distance):
    count = lax.axis_size(axis)
    perm = [(i, i ^ distance) for i in range(count)]
    return jnp.concatenate([piece, lax.ppermute(piece, axis, perm)], axis=0)


def ring_gather(piece, axis):
    count = lax.axis_size(axis)
    to_right = [(i, (i + 1) % count) for i in range(count)]
    to_left = [(i, (i - 1) % count) for i in range(count)]
    pieces = [piece]
    from_left = from_right = piece
    for step in range(1, count // 2 + 1):
        from_left = lax.ppermute(from_left, axis, to_right)
        pieces.append(from_left)
        if 2 * step < count:
            from_right = lax.ppermute(from_right, axis, to_left)
            pieces.append(from_right)
    return jnp.stack(pieces)


def pair_gather(piece, axis):
    return jnp.concatenate([piece, lax.ppermute(piece, axis, SWAP)], axis=0)


def shards(features, cotangents, labels, diff_mask, class_weight, owners, momentum):
    dp_count = lax.axis_size(DP)
    z_count = lax.axis_size("z")
    tensor_count = lax.axis_size(TP)
    local_tokens = cotangents.shape[0]
    scaled = weigh(cotangents, labels, diff_mask, class_weight, local_tokens * dp_count)
    heads_here = owners.shape[0]
    head_width = cotangents.shape[1] // heads_here
    feature_rows = features.shape[0]
    block_rows = feature_rows * tensor_count // dp_count
    sub_blocks = feature_rows // block_rows
    inverse = invert(owners)
    z = lax.axis_index("z")
    xl = lax.axis_index("xl")
    c = lax.axis_index("c")
    xh = lax.axis_index("xh")

    y_count = lax.axis_size("y")
    half, quarter = dp_count // 2, dp_count // 4
    quarter_rows = block_rows // 4
    pair_rows = pair_gather(features, "xh")
    y = lax.axis_index("y")
    ring_pieces = ring_gather(scaled, "y")
    head = jnp.arange(y_count, dtype=jnp.int32)
    ahead = (head - y) % y_count
    behind = (y - head) % y_count
    slot = jnp.where(ahead == 0, 0, jnp.where(ahead < behind, 2 * ahead, 2 * behind - 1))
    heads_y = jnp.transpose(jnp.take(ring_pieces, slot, axis=0), (1, 0, 2)).reshape(
        local_tokens, y_count * head_width
    )
    pair_blocks = 2 * sub_blocks
    group_rows = pair_blocks * quarter_rows
    position = jnp.arange(2 * feature_rows, dtype=jnp.int32)
    group = position // group_rows
    within = position % group_rows
    j = within // quarter_rows
    r = within % quarter_rows
    quarter_xl = jnp.where(group % 2 == 0, xl, 1 - xl)
    quarter_c = jnp.where(group < 2, c, 1 - c)
    u = 2 * quarter_xl + quarter_c
    shard_slot = jnp.where(j // sub_blocks == xh, 0, 1)
    source_row = shard_slot * feature_rows + (j % sub_blocks) * block_rows + u * quarter_rows + r
    arranged = jnp.take(pair_rows, source_row, axis=0)
    partial = jnp.dot(arranged, heads_y, preferred_element_type=jnp.float32).reshape(
        2 * feature_rows, y_count, head_width
    )
    kept = pair_sum_scatter(partial, "c")
    kept = pair_sum_scatter(kept, "xl")
    quarters = lax.all_to_all(kept, "y", split_axis=1, concat_axis=0, tiled=True).reshape(
        dp_count, quarter_rows, head_width
    )
    per_z = dp_count // z_count
    in_owner_order = jnp.take(quarters, inverse[0], axis=0)
    from_z = lax.all_to_all(in_owner_order, "z", split_axis=0, concat_axis=0, tiled=True)
    local_owners = jnp.sum(
        from_z.reshape(z_count, per_z * quarter_rows, head_width), axis=0
    )
    own_block = lax.all_to_all(
        local_owners, ("xl", "c"), split_axis=0, concat_axis=0, tiled=True
    ).reshape(block_rows, heads_here, head_width)

    previous = momentum.reshape(block_rows, heads_here, head_width)
    new_momentum = decay_rate * previous + own_block
    nesterov = own_block + decay_rate * new_momentum
    ortho = orthogonalize(nesterov)
    own_update = (
        (ortho * math.sqrt(block_rows))
        .astype(jnp.bfloat16)
        .reshape(block_rows, heads_here * head_width)
    )
    gathered = lax.all_to_all(
        jnp.broadcast_to(own_update[None], (z_count,) + own_update.shape),
        "z",
        split_axis=0,
        concat_axis=0,
        tiled=True,
    ).reshape(z_count * block_rows, heads_here * head_width)
    gathered = pair_gather(gathered, "xl")
    gathered = pair_gather(gathered, "c")
    d = jnp.arange(dp_count, dtype=jnp.int32)
    update_position = (
        jnp.where(d % 2 == c, 0, half) + jnp.where((d // 2) % 2 == xl, 0, quarter) + d // 4
    )
    placed = reorder(
        gathered.reshape(dp_count, block_rows, heads_here, head_width), update_position[owners]
    )
    return (
        placed.reshape(dp_count * block_rows, heads_here * head_width),
        new_momentum.reshape(block_rows, heads_here * head_width),
    )


def solution(mesh):
    dp_size, tp_size = mesh.shape["dp"], mesh.shape["tensor"]
    fine = Mesh(mesh.devices.reshape(dp_size // 4, 2, 2, tp_size // 2, 2), DP + TP)
    in_specs = (
        P(TP, DP),
        P(DP, TP),
        P(DP),
        P(DP),
        P(),
        P(TP, None),
        P(DP, TP),
    )
    out_specs = (P(None, TP), P(DP, TP))
    return jax.shard_map(shards, mesh=fine, in_specs=in_specs, out_specs=out_specs, check_vma=False)
```

```python
import math

import jax
import jax.numpy as jnp
from jax import lax
from jax.sharding import Mesh, PartitionSpec as P

ITERS = 5


decay_rate = 0.95
quintic_first = 3.4445
quintic_second = -4.775
quintic_third = 2.0315
norm_epsilon = 1e-07

DP = ("z", "xl", "c")
TP = ("y", "xh")
SWAP = [(0, 1), (1, 0)]


def weigh(cotangents, labels, diff_mask, class_weight, total_tokens):
    classes = jnp.arange(class_weight.shape[0], dtype=jnp.int32)
    picked = (labels[:, None] == classes[None, :]).astype(jnp.float32)
    token_weight = diff_mask.astype(jnp.float32) * jnp.sum(picked * class_weight[None, :], axis=1)
    factor = token_weight / math.sqrt(total_tokens)
    return (cotangents.astype(jnp.float32) * factor[:, None]).astype(jnp.bfloat16)


def invert(owners):
    number = owners.shape[1]
    candidates = jnp.arange(number, dtype=jnp.int32)
    matches = owners[:, None, :] == candidates[None, :, None]
    return jnp.sum(jnp.where(matches, candidates[None, None, :], 0), axis=2)


def reorder(blocks, lookup):
    return jnp.take_along_axis(blocks, jnp.transpose(lookup)[:, None, :, None], axis=0)


def orthogonalize(nesterov):
    frobenius = jnp.sqrt(jnp.sum(nesterov * nesterov, axis=(-3, -1), keepdims=True)) + norm_epsilon
    iterate = nesterov / frobenius
    for step in range(ITERS):
        gram_matrix = jnp.einsum(
            "...rhc,...rhd->...hcd", iterate, iterate, precision=lax.Precision.HIGHEST
        )
        poly_matrix = quintic_second * gram_matrix + quintic_third * jnp.einsum(
            "...hcd,...hde->...hce", gram_matrix, gram_matrix, precision=lax.Precision.HIGHEST
        )
        iterate = quintic_first * iterate + jnp.einsum(
            "...rhc,...hcd->...rhd", iterate, poly_matrix, precision=lax.Precision.HIGHEST
        )
    return iterate


def pair_sum_scatter(blocks, axis):
    half = blocks.shape[0] // 2
    return blocks[:half] + lax.ppermute(blocks[half:], axis, SWAP)


def xor_sum_scatter(blocks, axis, distance):
    half = blocks.shape[0] // 2
    count = lax.axis_size(axis)
    perm = [(i, i ^ distance) for i in range(count)]
    return blocks[:half] + lax.ppermute(blocks[half:], axis, perm)


def xor_gather(piece, axis, distance):
    count = lax.axis_size(axis)
    perm = [(i, i ^ distance) for i in range(count)]
    return jnp.concatenate([piece, lax.ppermute(piece, axis, perm)], axis=0)


def ring_gather(piece, axis):
    count = lax.axis_size(axis)
    to_right = [(i, (i + 1) % count) for i in range(count)]
    to_left = [(i, (i - 1) % count) for i in range(count)]
    pieces = [piece]
    from_left = from_right = piece
    for step in range(1, count // 2 + 1):
        from_left = lax.ppermute(from_left, axis, to_right)
        pieces.append(from_left)
        if 2 * step < count:
            from_right = lax.ppermute(from_right, axis, to_left)
            pieces.append(from_right)
    return jnp.stack(pieces)


def pair_gather(piece, axis):
    return jnp.concatenate([piece, lax.ppermute(piece, axis, SWAP)], axis=0)


def shards(features, cotangents, labels, diff_mask, class_weight, owners, momentum):
    dp_count = lax.axis_size(DP)
    z_count = lax.axis_size("z")
    tensor_count = lax.axis_size(TP)
    local_tokens = cotangents.shape[0]
    scaled = weigh(cotangents, labels, diff_mask, class_weight, local_tokens * dp_count)
    heads_here = owners.shape[0]
    head_width = cotangents.shape[1] // heads_here
    feature_rows = features.shape[0]
    block_rows = feature_rows * tensor_count // dp_count
    sub_blocks = feature_rows // block_rows
    inverse = invert(owners)
    z = lax.axis_index("z")
    xl = lax.axis_index("xl")
    c = lax.axis_index("c")
    xh = lax.axis_index("xh")

    y_count = lax.axis_size("y")
    half, quarter = dp_count // 2, dp_count // 4
    quarter_rows = block_rows // 4
    pair_rows = pair_gather(features, "xh")
    y = lax.axis_index("y")
    ring_pieces = ring_gather(scaled, "y")
    head = jnp.arange(y_count, dtype=jnp.int32)
    ahead = (head - y) % y_count
    behind = (y - head) % y_count
    slot = jnp.where(ahead == 0, 0, jnp.where(ahead < behind, 2 * ahead, 2 * behind - 1))
    heads_y = jnp.transpose(jnp.take(ring_pieces, slot, axis=0), (1, 0, 2)).reshape(
        local_tokens, y_count * head_width
    )
    pair_blocks = 2 * sub_blocks
    group_rows = pair_blocks * quarter_rows
    position = jnp.arange(2 * feature_rows, dtype=jnp.int32)
    group = position // group_rows
    within = position % group_rows
    j = within // quarter_rows
    r = within % quarter_rows
    quarter_xl = jnp.where(group % 2 == 0, xl, 1 - xl)
    quarter_c = jnp.where(group < 2, c, 1 - c)
    u = 2 * quarter_xl + quarter_c
    shard_slot = jnp.where(j // sub_blocks == xh, 0, 1)
    source_row = shard_slot * feature_rows + (j % sub_blocks) * block_rows + u * quarter_rows + r
    arranged = jnp.take(pair_rows, source_row, axis=0)
    partial = jnp.dot(arranged, heads_y, preferred_element_type=jnp.float32).reshape(
        2 * feature_rows, y_count, head_width
    )
    kept = pair_sum_scatter(partial, "c")
    kept = pair_sum_scatter(kept, "xl")
    quarters = lax.all_to_all(kept, "y", split_axis=1, concat_axis=0, tiled=True).reshape(
        dp_count, quarter_rows, head_width
    )
    in_owner_order = jnp.take(quarters, inverse[0], axis=0)
    from_all = lax.all_to_all(in_owner_order, DP, split_axis=0, concat_axis=0, tiled=True)
    own_block = jnp.sum(
        from_all.reshape(z_count, dp_count // z_count, quarter_rows, head_width), axis=0
    ).reshape(block_rows, heads_here, head_width)

    previous = momentum.reshape(block_rows, heads_here, head_width)
    new_momentum = decay_rate * previous + own_block
    nesterov = own_block + decay_rate * new_momentum
    ortho = orthogonalize(nesterov)
    own_update = (
        (ortho * math.sqrt(block_rows))
        .astype(jnp.bfloat16)
        .reshape(block_rows, heads_here * head_width)
    )
    gathered = lax.all_to_all(
        jnp.broadcast_to(own_update[None], (z_count,) + own_update.shape),
        "z",
        split_axis=0,
        concat_axis=0,
        tiled=True,
    ).reshape(z_count * block_rows, heads_here * head_width)
    gathered = pair_gather(gathered, "xl")
    gathered = pair_gather(gathered, "c")
    d = jnp.arange(dp_count, dtype=jnp.int32)
    update_position = (
        jnp.where(d % 2 == c, 0, half) + jnp.where((d // 2) % 2 == xl, 0, quarter) + d // 4
    )
    placed = reorder(
        gathered.reshape(dp_count, block_rows, heads_here, head_width), update_position[owners]
    )
    return (
        placed.reshape(dp_count * block_rows, heads_here * head_width),
        new_momentum.reshape(block_rows, heads_here * head_width),
    )


def solution(mesh):
    dp_size, tp_size = mesh.shape["dp"], mesh.shape["tensor"]
    fine = Mesh(mesh.devices.reshape(dp_size // 4, 2, 2, tp_size // 2, 2), DP + TP)
    in_specs = (
        P(TP, DP),
        P(DP, TP),
        P(DP),
        P(DP),
        P(),
        P(TP, None),
        P(DP, TP),
    )
    out_specs = (P(None, TP), P(DP, TP))
    return jax.shard_map(shards, mesh=fine, in_specs=in_specs, out_specs=out_specs, check_vma=False)
```

```python
import math

import jax
import jax.numpy as jnp
from jax import lax
from jax.sharding import Mesh, PartitionSpec as P

ITERS = 5


decay_rate = 0.95
quintic_first = 3.4445
quintic_second = -4.775
quintic_third = 2.0315
norm_epsilon = 1e-07

DP = ("z", "xl", "c")
TP = ("y", "xh")
SWAP = [(0, 1), (1, 0)]


def weigh(cotangents, labels, diff_mask, class_weight, total_tokens):
    classes = jnp.arange(class_weight.shape[0], dtype=jnp.int32)
    picked = (labels[:, None] == classes[None, :]).astype(jnp.float32)
    token_weight = diff_mask.astype(jnp.float32) * jnp.sum(picked * class_weight[None, :], axis=1)
    factor = token_weight / math.sqrt(total_tokens)
    return (cotangents.astype(jnp.float32) * factor[:, None]).astype(jnp.bfloat16)


def invert(owners):
    number = owners.shape[1]
    candidates = jnp.arange(number, dtype=jnp.int32)
    matches = owners[:, None, :] == candidates[None, :, None]
    return jnp.sum(jnp.where(matches, candidates[None, None, :], 0), axis=2)


def reorder(blocks, lookup):
    return jnp.take_along_axis(blocks, jnp.transpose(lookup)[:, None, :, None], axis=0)


def orthogonalize(nesterov):
    frobenius = jnp.sqrt(jnp.sum(nesterov * nesterov, axis=(-3, -1), keepdims=True)) + norm_epsilon
    iterate = nesterov / frobenius
    for step in range(ITERS):
        gram_matrix = jnp.einsum(
            "...rhc,...rhd->...hcd", iterate, iterate, precision=lax.Precision.HIGHEST
        )
        poly_matrix = quintic_second * gram_matrix + quintic_third * jnp.einsum(
            "...hcd,...hde->...hce", gram_matrix, gram_matrix, precision=lax.Precision.HIGHEST
        )
        iterate = quintic_first * iterate + jnp.einsum(
            "...rhc,...hcd->...rhd", iterate, poly_matrix, precision=lax.Precision.HIGHEST
        )
    return iterate


def pair_sum_scatter(blocks, axis):
    half = blocks.shape[0] // 2
    return blocks[:half] + lax.ppermute(blocks[half:], axis, SWAP)


def xor_sum_scatter(blocks, axis, distance):
    half = blocks.shape[0] // 2
    count = lax.axis_size(axis)
    perm = [(i, i ^ distance) for i in range(count)]
    return blocks[:half] + lax.ppermute(blocks[half:], axis, perm)


def xor_gather(piece, axis, distance):
    count = lax.axis_size(axis)
    perm = [(i, i ^ distance) for i in range(count)]
    return jnp.concatenate([piece, lax.ppermute(piece, axis, perm)], axis=0)


def ring_gather(piece, axis):
    count = lax.axis_size(axis)
    to_right = [(i, (i + 1) % count) for i in range(count)]
    to_left = [(i, (i - 1) % count) for i in range(count)]
    pieces = [piece]
    from_left = from_right = piece
    for step in range(1, count // 2 + 1):
        from_left = lax.ppermute(from_left, axis, to_right)
        pieces.append(from_left)
        if 2 * step < count:
            from_right = lax.ppermute(from_right, axis, to_left)
            pieces.append(from_right)
    return pieces


def pair_gather(piece, axis):
    return jnp.concatenate([piece, lax.ppermute(piece, axis, SWAP)], axis=0)


def shards(features, cotangents, labels, diff_mask, class_weight, owners, momentum):
    dp_count = lax.axis_size(DP)
    z_count = lax.axis_size("z")
    tensor_count = lax.axis_size(TP)
    local_tokens = cotangents.shape[0]
    scaled = weigh(cotangents, labels, diff_mask, class_weight, local_tokens * dp_count)
    heads_here = owners.shape[0]
    head_width = cotangents.shape[1] // heads_here
    feature_rows = features.shape[0]
    block_rows = feature_rows * tensor_count // dp_count
    sub_blocks = feature_rows // block_rows
    inverse = invert(owners)
    z = lax.axis_index("z")
    xl = lax.axis_index("xl")
    c = lax.axis_index("c")
    xh = lax.axis_index("xh")

    y_count = lax.axis_size("y")
    half, quarter = dp_count // 2, dp_count // 4
    quarter_rows = block_rows // 4
    pair_rows = pair_gather(features, "xh")
    y = lax.axis_index("y")
    ring_pieces = ring_gather(scaled, "y")
    pair_blocks = 2 * sub_blocks
    group_rows = pair_blocks * quarter_rows
    position = jnp.arange(2 * feature_rows, dtype=jnp.int32)
    group = position // group_rows
    within = position % group_rows
    j = within // quarter_rows
    r = within % quarter_rows
    quarter_xl = jnp.where(group % 2 == 0, xl, 1 - xl)
    quarter_c = jnp.where(group < 2, c, 1 - c)
    u = 2 * quarter_xl + quarter_c
    shard_slot = jnp.where(j // sub_blocks == xh, 0, 1)
    source_row = shard_slot * feature_rows + (j % sub_blocks) * block_rows + u * quarter_rows + r
    arranged = jnp.take(pair_rows, source_row, axis=0)

    def reduced_heads(pieces):
        partial = jnp.dot(
            arranged, jnp.concatenate(pieces, axis=1), preferred_element_type=jnp.float32
        ).reshape(2 * feature_rows, len(pieces), head_width)
        kept = pair_sum_scatter(partial, "c")
        return pair_sum_scatter(kept, "xl")

    early = 2 * 2 + 1
    kept_ring_order = jnp.concatenate(
        [reduced_heads(ring_pieces[:early]), reduced_heads(ring_pieces[early:])], axis=1
    )
    head = jnp.arange(y_count, dtype=jnp.int32)
    ahead = (head - y) % y_count
    behind = (y - head) % y_count
    slot = jnp.where(ahead == 0, 0, jnp.where(ahead < behind, 2 * ahead, 2 * behind - 1))
    kept = jnp.take(kept_ring_order, slot, axis=1)
    quarters = lax.all_to_all(kept, "y", split_axis=1, concat_axis=0, tiled=True).reshape(
        dp_count, quarter_rows, head_width
    )
    in_owner_order = jnp.take(quarters, inverse[0], axis=0)
    from_all = lax.all_to_all(in_owner_order, DP, split_axis=0, concat_axis=0, tiled=True)
    own_block = jnp.sum(
        from_all.reshape(z_count, dp_count // z_count, quarter_rows, head_width), axis=0
    ).reshape(block_rows, heads_here, head_width)

    previous = momentum.reshape(block_rows, heads_here, head_width)
    new_momentum = decay_rate * previous + own_block
    nesterov = own_block + decay_rate * new_momentum
    ortho = orthogonalize(nesterov)
    own_update = (
        (ortho * math.sqrt(block_rows))
        .astype(jnp.bfloat16)
        .reshape(block_rows, heads_here * head_width)
    )
    gathered = lax.all_to_all(
        jnp.broadcast_to(own_update[None], (z_count,) + own_update.shape),
        "z",
        split_axis=0,
        concat_axis=0,
        tiled=True,
    ).reshape(z_count * block_rows, heads_here * head_width)
    gathered = pair_gather(gathered, "xl")
    gathered = pair_gather(gathered, "c")
    d = jnp.arange(dp_count, dtype=jnp.int32)
    update_position = (
        jnp.where(d % 2 == c, 0, half) + jnp.where((d // 2) % 2 == xl, 0, quarter) + d // 4
    )
    placed = reorder(
        gathered.reshape(dp_count, block_rows, heads_here, head_width), update_position[owners]
    )
    return (
        placed.reshape(dp_count * block_rows, heads_here * head_width),
        new_momentum.reshape(block_rows, heads_here * head_width),
    )


def solution(mesh):
    dp_size, tp_size = mesh.shape["dp"], mesh.shape["tensor"]
    fine = Mesh(mesh.devices.reshape(dp_size // 4, 2, 2, tp_size // 2, 2), DP + TP)
    in_specs = (
        P(TP, DP),
        P(DP, TP),
        P(DP),
        P(DP),
        P(),
        P(TP, None),
        P(DP, TP),
    )
    out_specs = (P(None, TP), P(DP, TP))
    return jax.shard_map(shards, mesh=fine, in_specs=in_specs, out_specs=out_specs, check_vma=False)
```

```python
import math

import jax
import jax.numpy as jnp
from jax import lax
from jax.sharding import Mesh, PartitionSpec as P

ITERS = 5


decay_rate = 0.95
quintic_first = 3.4445
quintic_second = -4.775
quintic_third = 2.0315
norm_epsilon = 1e-07

DP = ("z", "xl", "c")
TP = ("y", "xh")
SWAP = [(0, 1), (1, 0)]


def weigh(cotangents, labels, diff_mask, class_weight, total_tokens):
    classes = jnp.arange(class_weight.shape[0], dtype=jnp.int32)
    picked = (labels[:, None] == classes[None, :]).astype(jnp.float32)
    token_weight = diff_mask.astype(jnp.float32) * jnp.sum(picked * class_weight[None, :], axis=1)
    factor = token_weight / math.sqrt(total_tokens)
    return (cotangents.astype(jnp.float32) * factor[:, None]).astype(jnp.bfloat16)


def invert(owners):
    number = owners.shape[1]
    candidates = jnp.arange(number, dtype=jnp.int32)
    matches = owners[:, None, :] == candidates[None, :, None]
    return jnp.sum(jnp.where(matches, candidates[None, None, :], 0), axis=2)


def reorder(blocks, lookup):
    return jnp.take_along_axis(blocks, jnp.transpose(lookup)[:, None, :, None], axis=0)


def orthogonalize(nesterov):
    frobenius = jnp.sqrt(jnp.sum(nesterov * nesterov, axis=(-3, -1), keepdims=True)) + norm_epsilon
    iterate = nesterov / frobenius
    for step in range(ITERS):
        gram_matrix = jnp.einsum(
            "...rhc,...rhd->...hcd", iterate, iterate, precision=lax.Precision.HIGHEST
        )
        poly_matrix = quintic_second * gram_matrix + quintic_third * jnp.einsum(
            "...hcd,...hde->...hce", gram_matrix, gram_matrix, precision=lax.Precision.HIGHEST
        )
        iterate = quintic_first * iterate + jnp.einsum(
            "...rhc,...hcd->...rhd", iterate, poly_matrix, precision=lax.Precision.HIGHEST
        )
    return iterate


def pair_sum_scatter(blocks, axis):
    half = blocks.shape[0] // 2
    return blocks[:half] + lax.ppermute(blocks[half:], axis, SWAP)


def xor_sum_scatter(blocks, axis, distance):
    half = blocks.shape[0] // 2
    count = lax.axis_size(axis)
    perm = [(i, i ^ distance) for i in range(count)]
    return blocks[:half] + lax.ppermute(blocks[half:], axis, perm)


def xor_gather(piece, axis, distance):
    count = lax.axis_size(axis)
    perm = [(i, i ^ distance) for i in range(count)]
    return jnp.concatenate([piece, lax.ppermute(piece, axis, perm)], axis=0)


def ring_gather(piece, axis):
    count = lax.axis_size(axis)
    to_right = [(i, (i + 1) % count) for i in range(count)]
    to_left = [(i, (i - 1) % count) for i in range(count)]
    pieces = [piece]
    from_left = from_right = piece
    for step in range(1, count // 2 + 1):
        from_left = lax.ppermute(from_left, axis, to_right)
        pieces.append(from_left)
        if 2 * step < count:
            from_right = lax.ppermute(from_right, axis, to_left)
            pieces.append(from_right)
    return pieces


def pair_gather(piece, axis):
    return jnp.concatenate([piece, lax.ppermute(piece, axis, SWAP)], axis=0)


def shards(features, cotangents, labels, diff_mask, class_weight, owners, momentum):
    dp_count = lax.axis_size(DP)
    z_count = lax.axis_size("z")
    tensor_count = lax.axis_size(TP)
    local_tokens = cotangents.shape[0]
    scaled = weigh(cotangents, labels, diff_mask, class_weight, local_tokens * dp_count)
    heads_here = owners.shape[0]
    head_width = cotangents.shape[1] // heads_here
    feature_rows = features.shape[0]
    block_rows = feature_rows * tensor_count // dp_count
    sub_blocks = feature_rows // block_rows
    inverse = invert(owners)
    z = lax.axis_index("z")
    xl = lax.axis_index("xl")
    c = lax.axis_index("c")
    xh = lax.axis_index("xh")

    y_count = lax.axis_size("y")
    half, quarter = dp_count // 2, dp_count // 4
    quarter_rows = block_rows // 4
    pair_rows = pair_gather(features, "xh")
    y = lax.axis_index("y")
    ring_pieces = ring_gather(scaled, "y")
    pair_blocks = 2 * sub_blocks
    group_rows = pair_blocks * quarter_rows
    position = jnp.arange(2 * feature_rows, dtype=jnp.int32)
    group = position // group_rows
    within = position % group_rows
    j = within // quarter_rows
    r = within % quarter_rows
    quarter_xl = jnp.where(group % 2 == 0, xl, 1 - xl)
    quarter_c = jnp.where(group < 2, c, 1 - c)
    u = 2 * quarter_xl + quarter_c
    shard_slot = jnp.where(j // sub_blocks == xh, 0, 1)
    source_row = shard_slot * feature_rows + (j % sub_blocks) * block_rows + u * quarter_rows + r
    arranged = jnp.take(pair_rows, source_row, axis=0)

    def reduced_heads(rows, pieces):
        partial = jnp.dot(
            rows, jnp.concatenate(pieces, axis=1), preferred_element_type=jnp.float32
        ).reshape(2 * feature_rows, len(pieces), head_width)
        kept = pair_sum_scatter(partial, "c")
        return pair_sum_scatter(kept, "xl")

    early = 2 * 2 + 1
    kept_early = reduced_heads(arranged, ring_pieces[:early])
    arranged_late, kept_early = lax.optimization_barrier((arranged, kept_early))
    kept_ring_order = jnp.concatenate(
        [kept_early, reduced_heads(arranged_late, ring_pieces[early:])], axis=1
    )
    head = jnp.arange(y_count, dtype=jnp.int32)
    ahead = (head - y) % y_count
    behind = (y - head) % y_count
    slot = jnp.where(ahead == 0, 0, jnp.where(ahead < behind, 2 * ahead, 2 * behind - 1))
    kept = jnp.take(kept_ring_order, slot, axis=1)
    quarters = lax.all_to_all(kept, "y", split_axis=1, concat_axis=0, tiled=True).reshape(
        dp_count, quarter_rows, head_width
    )
    in_owner_order = jnp.take(quarters, inverse[0], axis=0)
    from_all = lax.all_to_all(in_owner_order, DP, split_axis=0, concat_axis=0, tiled=True)
    own_block = jnp.sum(
        from_all.reshape(z_count, dp_count // z_count, quarter_rows, head_width), axis=0
    ).reshape(block_rows, heads_here, head_width)

    previous = momentum.reshape(block_rows, heads_here, head_width)
    new_momentum = decay_rate * previous + own_block
    nesterov = own_block + decay_rate * new_momentum
    ortho = orthogonalize(nesterov)
    own_update = (
        (ortho * math.sqrt(block_rows))
        .astype(jnp.bfloat16)
        .reshape(block_rows, heads_here * head_width)
    )
    gathered = lax.all_to_all(
        jnp.broadcast_to(own_update[None], (z_count,) + own_update.shape),
        "z",
        split_axis=0,
        concat_axis=0,
        tiled=True,
    ).reshape(z_count * block_rows, heads_here * head_width)
    gathered = pair_gather(gathered, "xl")
    gathered = pair_gather(gathered, "c")
    d = jnp.arange(dp_count, dtype=jnp.int32)
    update_position = (
        jnp.where(d % 2 == c, 0, half) + jnp.where((d // 2) % 2 == xl, 0, quarter) + d // 4
    )
    placed = reorder(
        gathered.reshape(dp_count, block_rows, heads_here, head_width), update_position[owners]
    )
    return (
        placed.reshape(dp_count * block_rows, heads_here * head_width),
        new_momentum.reshape(block_rows, heads_here * head_width),
    )


def solution(mesh):
    dp_size, tp_size = mesh.shape["dp"], mesh.shape["tensor"]
    fine = Mesh(mesh.devices.reshape(dp_size // 4, 2, 2, tp_size // 2, 2), DP + TP)
    in_specs = (
        P(TP, DP),
        P(DP, TP),
        P(DP),
        P(DP),
        P(),
        P(TP, None),
        P(DP, TP),
    )
    out_specs = (P(None, TP), P(DP, TP))
    return jax.shard_map(shards, mesh=fine, in_specs=in_specs, out_specs=out_specs, check_vma=False)
```

```python
import math

import jax
import jax.numpy as jnp
from jax import lax
from jax.sharding import Mesh, PartitionSpec as P

ITERS = 5


decay_rate = 0.95
quintic_first = 3.4445
quintic_second = -4.775
quintic_third = 2.0315
norm_epsilon = 1e-07

DP = ("z", "xl", "c")
TP = ("y", "xh")
SWAP = [(0, 1), (1, 0)]


def token_factor(labels, diff_mask, class_weight, total_tokens):
    classes = jnp.arange(class_weight.shape[0], dtype=jnp.int32)
    picked = (labels[:, None] == classes[None, :]).astype(jnp.float32)
    token_weight = diff_mask.astype(jnp.float32) * jnp.sum(picked * class_weight[None, :], axis=1)
    return token_weight / math.sqrt(total_tokens)


def weigh(cotangents, factor):
    return (cotangents.astype(jnp.float32) * factor[:, None]).astype(jnp.bfloat16)


def invert(owners):
    number = owners.shape[1]
    candidates = jnp.arange(number, dtype=jnp.int32)
    matches = owners[:, None, :] == candidates[None, :, None]
    return jnp.sum(jnp.where(matches, candidates[None, None, :], 0), axis=2)


def reorder(blocks, lookup):
    return jnp.take_along_axis(blocks, jnp.transpose(lookup)[:, None, :, None], axis=0)


def orthogonalize(nesterov):
    frobenius = jnp.sqrt(jnp.sum(nesterov * nesterov, axis=(-3, -1), keepdims=True)) + norm_epsilon
    iterate = nesterov / frobenius
    for step in range(ITERS):
        gram_matrix = jnp.einsum(
            "...rhc,...rhd->...hcd", iterate, iterate, precision=lax.Precision.HIGHEST
        )
        poly_matrix = quintic_second * gram_matrix + quintic_third * jnp.einsum(
            "...hcd,...hde->...hce", gram_matrix, gram_matrix, precision=lax.Precision.HIGHEST
        )
        iterate = quintic_first * iterate + jnp.einsum(
            "...rhc,...hcd->...rhd", iterate, poly_matrix, precision=lax.Precision.HIGHEST
        )
    return iterate


def pair_sum_scatter(blocks, axis):
    half = blocks.shape[0] // 2
    return blocks[:half] + lax.ppermute(blocks[half:], axis, SWAP)


def xor_sum_scatter(blocks, axis, distance):
    half = blocks.shape[0] // 2
    count = lax.axis_size(axis)
    perm = [(i, i ^ distance) for i in range(count)]
    return blocks[:half] + lax.ppermute(blocks[half:], axis, perm)


def xor_gather(piece, axis, distance):
    count = lax.axis_size(axis)
    perm = [(i, i ^ distance) for i in range(count)]
    return jnp.concatenate([piece, lax.ppermute(piece, axis, perm)], axis=0)


def ring_gather(piece, axis):
    count = lax.axis_size(axis)
    to_right = [(i, (i + 1) % count) for i in range(count)]
    to_left = [(i, (i - 1) % count) for i in range(count)]
    pieces = [piece]
    from_left = from_right = piece
    for step in range(1, count // 2 + 1):
        from_left = lax.ppermute(from_left, axis, to_right)
        pieces.append(from_left)
        if 2 * step < count:
            from_right = lax.ppermute(from_right, axis, to_left)
            pieces.append(from_right)
    return pieces


def pair_gather(piece, axis):
    return jnp.concatenate([piece, lax.ppermute(piece, axis, SWAP)], axis=0)


def shards(features, cotangents, labels, diff_mask, class_weight, owners, momentum):
    dp_count = lax.axis_size(DP)
    z_count = lax.axis_size("z")
    tensor_count = lax.axis_size(TP)
    local_tokens = cotangents.shape[0]
    factor = token_factor(labels, diff_mask, class_weight, local_tokens * dp_count)
    heads_here = owners.shape[0]
    head_width = cotangents.shape[1] // heads_here
    feature_rows = features.shape[0]
    block_rows = feature_rows * tensor_count // dp_count
    sub_blocks = feature_rows // block_rows
    inverse = invert(owners)
    z = lax.axis_index("z")
    xl = lax.axis_index("xl")
    c = lax.axis_index("c")
    xh = lax.axis_index("xh")

    y_count = lax.axis_size("y")
    half, quarter = dp_count // 2, dp_count // 4
    quarter_rows = block_rows // 4
    pair_rows = pair_gather(features, "xh")
    y = lax.axis_index("y")
    ring_pieces = [weigh(piece, factor) for piece in ring_gather(cotangents, "y")]
    pair_blocks = 2 * sub_blocks
    group_rows = pair_blocks * quarter_rows
    position = jnp.arange(2 * feature_rows, dtype=jnp.int32)
    group = position // group_rows
    within = position % group_rows
    j = within // quarter_rows
    r = within % quarter_rows
    quarter_xl = jnp.where(group % 2 == 0, xl, 1 - xl)
    quarter_c = jnp.where(group < 2, c, 1 - c)
    u = 2 * quarter_xl + quarter_c
    shard_slot = jnp.where(j // sub_blocks == xh, 0, 1)
    source_row = shard_slot * feature_rows + (j % sub_blocks) * block_rows + u * quarter_rows + r
    arranged = jnp.take(pair_rows, source_row, axis=0)

    def reduced_heads(pieces):
        partial = jnp.dot(
            arranged, jnp.concatenate(pieces, axis=1), preferred_element_type=jnp.float32
        ).reshape(2 * feature_rows, len(pieces), head_width)
        kept = pair_sum_scatter(partial, "c")
        return pair_sum_scatter(kept, "xl")

    early = 2 * 2 + 1
    kept_ring_order = jnp.concatenate(
        [reduced_heads(ring_pieces[:early]), reduced_heads(ring_pieces[early:])], axis=1
    )
    head = jnp.arange(y_count, dtype=jnp.int32)
    ahead = (head - y) % y_count
    behind = (y - head) % y_count
    slot = jnp.where(ahead == 0, 0, jnp.where(ahead < behind, 2 * ahead, 2 * behind - 1))
    kept = jnp.take(kept_ring_order, slot, axis=1)
    quarters = lax.all_to_all(kept, "y", split_axis=1, concat_axis=0, tiled=True).reshape(
        dp_count, quarter_rows, head_width
    )
    in_owner_order = jnp.take(quarters, inverse[0], axis=0)
    from_all = lax.all_to_all(in_owner_order, DP, split_axis=0, concat_axis=0, tiled=True)
    own_block = jnp.sum(
        from_all.reshape(z_count, dp_count // z_count, quarter_rows, head_width), axis=0
    ).reshape(block_rows, heads_here, head_width)

    previous = momentum.reshape(block_rows, heads_here, head_width)
    new_momentum = decay_rate * previous + own_block
    nesterov = own_block + decay_rate * new_momentum
    ortho = orthogonalize(nesterov)
    own_update = (
        (ortho * math.sqrt(block_rows))
        .astype(jnp.bfloat16)
        .reshape(block_rows, heads_here * head_width)
    )
    gathered = lax.all_to_all(
        jnp.broadcast_to(own_update[None], (z_count,) + own_update.shape),
        "z",
        split_axis=0,
        concat_axis=0,
        tiled=True,
    ).reshape(z_count * block_rows, heads_here * head_width)
    gathered = pair_gather(gathered, "xl")
    gathered = pair_gather(gathered, "c")
    d = jnp.arange(dp_count, dtype=jnp.int32)
    update_position = (
        jnp.where(d % 2 == c, 0, half) + jnp.where((d // 2) % 2 == xl, 0, quarter) + d // 4
    )
    placed = reorder(
        gathered.reshape(dp_count, block_rows, heads_here, head_width), update_position[owners]
    )
    return (
        placed.reshape(dp_count * block_rows, heads_here * head_width),
        new_momentum.reshape(block_rows, heads_here * head_width),
    )


def solution(mesh):
    dp_size, tp_size = mesh.shape["dp"], mesh.shape["tensor"]
    fine = Mesh(mesh.devices.reshape(dp_size // 4, 2, 2, tp_size // 2, 2), DP + TP)
    in_specs = (
        P(TP, DP),
        P(DP, TP),
        P(DP),
        P(DP),
        P(),
        P(TP, None),
        P(DP, TP),
    )
    out_specs = (P(None, TP), P(DP, TP))
    return jax.shard_map(shards, mesh=fine, in_specs=in_specs, out_specs=out_specs, check_vma=False)
```

```python
import math

import jax
import jax.numpy as jnp
from jax import lax
from jax.sharding import Mesh, PartitionSpec as P

ITERS = 5


decay_rate = 0.95
quintic_first = 3.4445
quintic_second = -4.775
quintic_third = 2.0315
norm_epsilon = 1e-07

DP = ("z", "xl", "c")
TP = ("y", "xh")
SWAP = [(0, 1), (1, 0)]


def token_factor(labels, diff_mask, class_weight, total_tokens):
    classes = jnp.arange(class_weight.shape[0], dtype=jnp.int32)
    picked = (labels[:, None] == classes[None, :]).astype(jnp.float32)
    token_weight = diff_mask.astype(jnp.float32) * jnp.sum(picked * class_weight[None, :], axis=1)
    return token_weight / math.sqrt(total_tokens)


def weigh(cotangents, factor):
    return (cotangents.astype(jnp.float32) * factor[:, None]).astype(jnp.bfloat16)


def invert(owners):
    number = owners.shape[1]
    candidates = jnp.arange(number, dtype=jnp.int32)
    matches = owners[:, None, :] == candidates[None, :, None]
    return jnp.sum(jnp.where(matches, candidates[None, None, :], 0), axis=2)


def reorder(blocks, lookup):
    return jnp.take_along_axis(blocks, jnp.transpose(lookup)[:, None, :, None], axis=0)


def orthogonalize(nesterov):
    frobenius = jnp.sqrt(jnp.sum(nesterov * nesterov, axis=(-3, -1), keepdims=True)) + norm_epsilon
    iterate = nesterov / frobenius
    for step in range(ITERS):
        gram_matrix = jnp.einsum(
            "...rhc,...rhd->...hcd", iterate, iterate, precision=lax.Precision.HIGHEST
        )
        poly_matrix = quintic_second * gram_matrix + quintic_third * jnp.einsum(
            "...hcd,...hde->...hce", gram_matrix, gram_matrix, precision=lax.Precision.HIGHEST
        )
        iterate = quintic_first * iterate + jnp.einsum(
            "...rhc,...hcd->...rhd", iterate, poly_matrix, precision=lax.Precision.HIGHEST
        )
    return iterate


def pair_sum_scatter(blocks, axis):
    half = blocks.shape[0] // 2
    return blocks[:half] + lax.ppermute(blocks[half:], axis, SWAP)


def xor_sum_scatter(blocks, axis, distance):
    half = blocks.shape[0] // 2
    count = lax.axis_size(axis)
    perm = [(i, i ^ distance) for i in range(count)]
    return blocks[:half] + lax.ppermute(blocks[half:], axis, perm)


def xor_gather(piece, axis, distance):
    count = lax.axis_size(axis)
    perm = [(i, i ^ distance) for i in range(count)]
    return jnp.concatenate([piece, lax.ppermute(piece, axis, perm)], axis=0)


def ring_gather(piece, axis):
    count = lax.axis_size(axis)
    to_right = [(i, (i + 1) % count) for i in range(count)]
    to_left = [(i, (i - 1) % count) for i in range(count)]
    pieces = [piece]
    from_left = from_right = piece
    for step in range(1, count // 2 + 1):
        from_left = lax.ppermute(from_left, axis, to_right)
        pieces.append(from_left)
        if 2 * step < count:
            from_right = lax.ppermute(from_right, axis, to_left)
            pieces.append(from_right)
    return pieces


def pair_gather(piece, axis):
    return jnp.concatenate([piece, lax.ppermute(piece, axis, SWAP)], axis=0)


def shards(features, cotangents, labels, diff_mask, class_weight, owners, momentum):
    dp_count = lax.axis_size(DP)
    z_count = lax.axis_size("z")
    tensor_count = lax.axis_size(TP)
    local_tokens = cotangents.shape[0]
    factor = token_factor(labels, diff_mask, class_weight, local_tokens * dp_count)
    heads_here = owners.shape[0]
    head_width = cotangents.shape[1] // heads_here
    feature_rows = features.shape[0]
    block_rows = feature_rows * tensor_count // dp_count
    sub_blocks = feature_rows // block_rows
    inverse = invert(owners)
    z = lax.axis_index("z")
    xl = lax.axis_index("xl")
    c = lax.axis_index("c")
    xh = lax.axis_index("xh")

    y_count = lax.axis_size("y")
    half, quarter = dp_count // 2, dp_count // 4
    quarter_rows = block_rows // 4
    pair_rows = pair_gather(features, "xh")
    y = lax.axis_index("y")
    ring_pieces = [weigh(piece, factor) for piece in ring_gather(cotangents, "y")]
    pair_blocks = 2 * sub_blocks
    group_rows = pair_blocks * quarter_rows
    position = jnp.arange(2 * feature_rows, dtype=jnp.int32)
    group = position // group_rows
    within = position % group_rows
    j = within // quarter_rows
    r = within % quarter_rows
    quarter_xl = jnp.where(group % 2 == 0, xl, 1 - xl)
    quarter_c = jnp.where(group < 2, c, 1 - c)
    u = 2 * quarter_xl + quarter_c
    shard_slot = jnp.where(j // sub_blocks == xh, 0, 1)
    source_row = shard_slot * feature_rows + (j % sub_blocks) * block_rows + u * quarter_rows + r
    arranged = jnp.take(pair_rows, source_row, axis=0)

    def core_reduced(rows, pieces):
        partial = jnp.dot(
            rows, jnp.concatenate(pieces, axis=1), preferred_element_type=jnp.float32
        ).reshape(2 * feature_rows, len(pieces), head_width)
        return pair_sum_scatter(partial, "c")

    early = 2 * 2 + 1
    early_core = core_reduced(arranged, ring_pieces[:early])
    arranged_late, early_core = lax.optimization_barrier((arranged, early_core))
    kept_ring_order = jnp.concatenate(
        [
            pair_sum_scatter(early_core, "xl"),
            pair_sum_scatter(core_reduced(arranged_late, ring_pieces[early:]), "xl"),
        ],
        axis=1,
    )
    head = jnp.arange(y_count, dtype=jnp.int32)
    ahead = (head - y) % y_count
    behind = (y - head) % y_count
    slot = jnp.where(ahead == 0, 0, jnp.where(ahead < behind, 2 * ahead, 2 * behind - 1))
    kept = jnp.take(kept_ring_order, slot, axis=1)
    quarters = lax.all_to_all(kept, "y", split_axis=1, concat_axis=0, tiled=True).reshape(
        dp_count, quarter_rows, head_width
    )
    in_owner_order = jnp.take(quarters, inverse[0], axis=0)
    from_all = lax.all_to_all(in_owner_order, DP, split_axis=0, concat_axis=0, tiled=True)
    own_block = jnp.sum(
        from_all.reshape(z_count, dp_count // z_count, quarter_rows, head_width), axis=0
    ).reshape(block_rows, heads_here, head_width)

    previous = momentum.reshape(block_rows, heads_here, head_width)
    new_momentum = decay_rate * previous + own_block
    nesterov = own_block + decay_rate * new_momentum
    ortho = orthogonalize(nesterov)
    own_update = (
        (ortho * math.sqrt(block_rows))
        .astype(jnp.bfloat16)
        .reshape(block_rows, heads_here * head_width)
    )
    gathered = lax.all_to_all(
        jnp.broadcast_to(own_update[None], (z_count,) + own_update.shape),
        "z",
        split_axis=0,
        concat_axis=0,
        tiled=True,
    ).reshape(z_count * block_rows, heads_here * head_width)
    gathered = pair_gather(gathered, "xl")
    gathered = pair_gather(gathered, "c")
    d = jnp.arange(dp_count, dtype=jnp.int32)
    update_position = (
        jnp.where(d % 2 == c, 0, half) + jnp.where((d // 2) % 2 == xl, 0, quarter) + d // 4
    )
    placed = reorder(
        gathered.reshape(dp_count, block_rows, heads_here, head_width), update_position[owners]
    )
    return (
        placed.reshape(dp_count * block_rows, heads_here * head_width),
        new_momentum.reshape(block_rows, heads_here * head_width),
    )


def solution(mesh):
    dp_size, tp_size = mesh.shape["dp"], mesh.shape["tensor"]
    fine = Mesh(mesh.devices.reshape(dp_size // 4, 2, 2, tp_size // 2, 2), DP + TP)
    in_specs = (
        P(TP, DP),
        P(DP, TP),
        P(DP),
        P(DP),
        P(),
        P(TP, None),
        P(DP, TP),
    )
    out_specs = (P(None, TP), P(DP, TP))
    return jax.shard_map(shards, mesh=fine, in_specs=in_specs, out_specs=out_specs, check_vma=False)
```

```python
import math

import jax
import jax.numpy as jnp
from jax import lax
from jax.sharding import Mesh, PartitionSpec as P

ITERS = 5


decay_rate = 0.95
quintic_first = 3.4445
quintic_second = -4.775
quintic_third = 2.0315
norm_epsilon = 1e-07

DP = ("z", "xl", "c")
TP = ("y", "xh")
SWAP = [(0, 1), (1, 0)]


def token_factor(labels, diff_mask, class_weight, total_tokens):
    classes = jnp.arange(class_weight.shape[0], dtype=jnp.int32)
    picked = (labels[:, None] == classes[None, :]).astype(jnp.float32)
    token_weight = diff_mask.astype(jnp.float32) * jnp.sum(picked * class_weight[None, :], axis=1)
    return token_weight / math.sqrt(total_tokens)


def weigh(cotangents, factor):
    return (cotangents.astype(jnp.float32) * factor[:, None]).astype(jnp.bfloat16)


def invert(owners):
    number = owners.shape[1]
    candidates = jnp.arange(number, dtype=jnp.int32)
    matches = owners[:, None, :] == candidates[None, :, None]
    return jnp.sum(jnp.where(matches, candidates[None, None, :], 0), axis=2)


def reorder(blocks, lookup):
    return jnp.take_along_axis(blocks, jnp.transpose(lookup)[:, None, :, None], axis=0)


def orthogonalize(nesterov):
    frobenius = jnp.sqrt(jnp.sum(nesterov * nesterov, axis=(-3, -1), keepdims=True)) + norm_epsilon
    iterate = nesterov / frobenius
    for step in range(ITERS):
        gram_matrix = jnp.einsum(
            "...rhc,...rhd->...hcd", iterate, iterate, precision=lax.Precision.HIGHEST
        )
        poly_matrix = quintic_second * gram_matrix + quintic_third * jnp.einsum(
            "...hcd,...hde->...hce", gram_matrix, gram_matrix, precision=lax.Precision.HIGHEST
        )
        iterate = quintic_first * iterate + jnp.einsum(
            "...rhc,...hcd->...rhd", iterate, poly_matrix, precision=lax.Precision.HIGHEST
        )
    return iterate


def pair_sum_scatter(blocks, axis):
    half = blocks.shape[0] // 2
    return blocks[:half] + lax.ppermute(blocks[half:], axis, SWAP)


def xor_sum_scatter(blocks, axis, distance):
    half = blocks.shape[0] // 2
    count = lax.axis_size(axis)
    perm = [(i, i ^ distance) for i in range(count)]
    return blocks[:half] + lax.ppermute(blocks[half:], axis, perm)


def xor_gather(piece, axis, distance):
    count = lax.axis_size(axis)
    perm = [(i, i ^ distance) for i in range(count)]
    return jnp.concatenate([piece, lax.ppermute(piece, axis, perm)], axis=0)


def ring_gather(piece, axis):
    count = lax.axis_size(axis)
    to_right = [(i, (i + 1) % count) for i in range(count)]
    to_left = [(i, (i - 1) % count) for i in range(count)]
    pieces = [piece]
    from_left = from_right = piece
    for step in range(1, count // 2 + 1):
        from_left = lax.ppermute(from_left, axis, to_right)
        pieces.append(from_left)
        if 2 * step < count:
            from_right = lax.ppermute(from_right, axis, to_left)
            pieces.append(from_right)
    return pieces


def pair_gather(piece, axis):
    return jnp.concatenate([piece, lax.ppermute(piece, axis, SWAP)], axis=0)


def shards(features, cotangents, labels, diff_mask, class_weight, owners, momentum):
    dp_count = lax.axis_size(DP)
    z_count = lax.axis_size("z")
    tensor_count = lax.axis_size(TP)
    local_tokens = cotangents.shape[0]
    factor = token_factor(labels, diff_mask, class_weight, local_tokens * dp_count)
    heads_here = owners.shape[0]
    head_width = cotangents.shape[1] // heads_here
    feature_rows = features.shape[0]
    block_rows = feature_rows * tensor_count // dp_count
    sub_blocks = feature_rows // block_rows
    inverse = invert(owners)
    z = lax.axis_index("z")
    xl = lax.axis_index("xl")
    c = lax.axis_index("c")
    xh = lax.axis_index("xh")

    y_count = lax.axis_size("y")
    half, quarter = dp_count // 2, dp_count // 4
    quarter_rows = block_rows // 4
    pair_rows = pair_gather(features, "xh")
    y = lax.axis_index("y")
    ring_pieces = [weigh(piece, factor) for piece in ring_gather(cotangents, "y")]
    pair_blocks = 2 * sub_blocks
    group_rows = pair_blocks * quarter_rows
    position = jnp.arange(2 * feature_rows, dtype=jnp.int32)
    group = position // group_rows
    within = position % group_rows
    j = within // quarter_rows
    r = within % quarter_rows
    quarter_xl = jnp.where(group % 2 == 0, xl, 1 - xl)
    quarter_c = jnp.where(group < 2, c, 1 - c)
    u = 2 * quarter_xl + quarter_c
    shard_slot = jnp.where(j // sub_blocks == xh, 0, 1)
    source_row = shard_slot * feature_rows + (j % sub_blocks) * block_rows + u * quarter_rows + r
    arranged = jnp.take(pair_rows, source_row, axis=0)

    def core_reduced(rows, pieces):
        partial = jnp.dot(
            rows, jnp.concatenate(pieces, axis=1), preferred_element_type=jnp.float32
        ).reshape(2 * feature_rows, len(pieces), head_width)
        return pair_sum_scatter(partial, "c")

    early = 2 * 2 + 1
    early_core = core_reduced(arranged, ring_pieces[:early])
    arranged_late, early_core = lax.optimization_barrier((arranged, early_core))
    kept_ring_order = jnp.concatenate(
        [
            pair_sum_scatter(early_core, "xl"),
            pair_sum_scatter(core_reduced(arranged_late, ring_pieces[early:]), "xl"),
        ],
        axis=1,
    )
    head = jnp.arange(y_count, dtype=jnp.int32)
    ahead = (head - y) % y_count
    behind = (y - head) % y_count
    slot = jnp.where(ahead == 0, 0, jnp.where(ahead < behind, 2 * ahead, 2 * behind - 1))
    kept = jnp.take(kept_ring_order, slot, axis=1)
    quarters = lax.all_to_all(kept, "y", split_axis=1, concat_axis=0, tiled=True).reshape(
        dp_count, quarter_rows, head_width
    )
    in_owner_order = jnp.take(quarters, inverse[0], axis=0)
    from_all = lax.all_to_all(in_owner_order, DP, split_axis=0, concat_axis=0, tiled=True)
    own_block = jnp.sum(
        from_all.reshape(z_count, dp_count // z_count, quarter_rows, head_width), axis=0
    ).reshape(block_rows, heads_here, head_width)

    previous = momentum.reshape(block_rows, heads_here, head_width)
    new_momentum = decay_rate * previous + own_block
    nesterov = own_block + decay_rate * new_momentum
    ortho = orthogonalize(nesterov)
    own_update = (
        (ortho * math.sqrt(block_rows))
        .astype(jnp.bfloat16)
        .reshape(block_rows, heads_here * head_width)
    )
    gathered = lax.all_to_all(
        jnp.broadcast_to(own_update[None], (z_count,) + own_update.shape),
        "z",
        split_axis=0,
        concat_axis=0,
        tiled=True,
    ).reshape(z_count * block_rows, heads_here * head_width)
    gathered = pair_gather(gathered, "xl")
    partner = lax.ppermute(gathered, "c", SWAP)
    d = jnp.arange(dp_count, dtype=jnp.int32)
    update_position = (
        jnp.where(d % 2 == c, 0, half) + jnp.where((d // 2) % 2 == xl, 0, quarter) + d // 4
    )
    source = update_position[owners[0]]
    slots = jnp.arange(half, dtype=jnp.int32)[None, :]
    pick_own = (source[:, None] == slots).astype(jnp.bfloat16)
    pick_partner = (source[:, None] == slots + half).astype(jnp.bfloat16)
    block_shape = (half, block_rows, heads_here * head_width)
    placed = (
        jnp.einsum(
            "bk,krc->brc", pick_own, gathered.reshape(block_shape), preferred_element_type=jnp.float32
        )
        + jnp.einsum(
            "bk,krc->brc", pick_partner, partner.reshape(block_shape), preferred_element_type=jnp.float32
        )
    ).astype(jnp.bfloat16)
    return (
        placed.reshape(dp_count * block_rows, heads_here * head_width),
        new_momentum.reshape(block_rows, heads_here * head_width),
    )


def solution(mesh):
    dp_size, tp_size = mesh.shape["dp"], mesh.shape["tensor"]
    fine = Mesh(mesh.devices.reshape(dp_size // 4, 2, 2, tp_size // 2, 2), DP + TP)
    in_specs = (
        P(TP, DP),
        P(DP, TP),
        P(DP),
        P(DP),
        P(),
        P(TP, None),
        P(DP, TP),
    )
    out_specs = (P(None, TP), P(DP, TP))
    return jax.shard_map(shards, mesh=fine, in_specs=in_specs, out_specs=out_specs, check_vma=False)
```

```python
import math

import jax
import jax.numpy as jnp
from jax import lax
from jax.sharding import Mesh, PartitionSpec as P

ITERS = 5


decay_rate = 0.95
quintic_first = 3.4445
quintic_second = -4.775
quintic_third = 2.0315
norm_epsilon = 1e-07

DP = ("z", "xl", "c")
TP = ("y", "xh")
SWAP = [(0, 1), (1, 0)]


def token_factor(labels, diff_mask, class_weight, total_tokens):
    classes = jnp.arange(class_weight.shape[0], dtype=jnp.int32)
    picked = (labels[:, None] == classes[None, :]).astype(jnp.float32)
    token_weight = diff_mask.astype(jnp.float32) * jnp.sum(picked * class_weight[None, :], axis=1)
    return token_weight / math.sqrt(total_tokens)


def weigh(cotangents, factor):
    return (cotangents.astype(jnp.float32) * factor[:, None]).astype(jnp.bfloat16)


def invert(owners):
    number = owners.shape[1]
    candidates = jnp.arange(number, dtype=jnp.int32)
    matches = owners[:, None, :] == candidates[None, :, None]
    return jnp.sum(jnp.where(matches, candidates[None, None, :], 0), axis=2)


def reorder(blocks, lookup):
    return jnp.take_along_axis(blocks, jnp.transpose(lookup)[:, None, :, None], axis=0)


def orthogonalize(nesterov):
    frobenius = jnp.sqrt(jnp.sum(nesterov * nesterov, axis=(-3, -1), keepdims=True)) + norm_epsilon
    iterate = nesterov / frobenius
    for step in range(ITERS):
        gram_matrix = jnp.einsum(
            "...rhc,...rhd->...hcd", iterate, iterate, precision=lax.Precision.HIGHEST
        )
        poly_matrix = quintic_second * gram_matrix + quintic_third * jnp.einsum(
            "...hcd,...hde->...hce", gram_matrix, gram_matrix, precision=lax.Precision.HIGHEST
        )
        iterate = quintic_first * iterate + jnp.einsum(
            "...rhc,...hcd->...rhd", iterate, poly_matrix, precision=lax.Precision.HIGHEST
        )
    return iterate


def pair_sum_scatter(blocks, axis):
    half = blocks.shape[0] // 2
    return blocks[:half] + lax.ppermute(blocks[half:], axis, SWAP)


def xor_sum_scatter(blocks, axis, distance):
    half = blocks.shape[0] // 2
    count = lax.axis_size(axis)
    perm = [(i, i ^ distance) for i in range(count)]
    return blocks[:half] + lax.ppermute(blocks[half:], axis, perm)


def xor_gather(piece, axis, distance):
    count = lax.axis_size(axis)
    perm = [(i, i ^ distance) for i in range(count)]
    return jnp.concatenate([piece, lax.ppermute(piece, axis, perm)], axis=0)


def ring_gather(piece, axis):
    count = lax.axis_size(axis)
    to_right = [(i, (i + 1) % count) for i in range(count)]
    to_left = [(i, (i - 1) % count) for i in range(count)]
    pieces = [piece]
    from_left = from_right = piece
    for step in range(1, count // 2 + 1):
        from_left = lax.ppermute(from_left, axis, to_right)
        pieces.append(from_left)
        if 2 * step < count:
            from_right = lax.ppermute(from_right, axis, to_left)
            pieces.append(from_right)
    return pieces


def pair_gather(piece, axis):
    return jnp.concatenate([piece, lax.ppermute(piece, axis, SWAP)], axis=0)


def shards(features, cotangents, labels, diff_mask, class_weight, owners, momentum):
    dp_count = lax.axis_size(DP)
    z_count = lax.axis_size("z")
    tensor_count = lax.axis_size(TP)
    local_tokens = cotangents.shape[0]
    factor = token_factor(labels, diff_mask, class_weight, local_tokens * dp_count)
    heads_here = owners.shape[0]
    head_width = cotangents.shape[1] // heads_here
    feature_rows = features.shape[0]
    block_rows = feature_rows * tensor_count // dp_count
    sub_blocks = feature_rows // block_rows
    inverse = invert(owners)
    z = lax.axis_index("z")
    xl = lax.axis_index("xl")
    c = lax.axis_index("c")
    xh = lax.axis_index("xh")

    y_count = lax.axis_size("y")
    half, quarter = dp_count // 2, dp_count // 4
    quarter_rows = block_rows // 4
    pair_rows = pair_gather(features, "xh")
    y = lax.axis_index("y")
    ring_pieces = [weigh(piece, factor) for piece in ring_gather(cotangents, "y")]
    pair_blocks = 2 * sub_blocks
    group_rows = pair_blocks * quarter_rows
    position = jnp.arange(2 * feature_rows, dtype=jnp.int32)
    group = position // group_rows
    within = position % group_rows
    j = within // quarter_rows
    r = within % quarter_rows
    quarter_xl = jnp.where(group % 2 == 0, xl, 1 - xl)
    quarter_c = jnp.where(group < 2, c, 1 - c)
    u = 2 * quarter_xl + quarter_c
    shard_slot = jnp.where(j // sub_blocks == xh, 0, 1)
    source_row = shard_slot * feature_rows + (j % sub_blocks) * block_rows + u * quarter_rows + r
    arranged = jnp.take(pair_rows, source_row, axis=0)

    def core_reduced(rows, pieces):
        partial = jnp.dot(
            rows, jnp.concatenate(pieces, axis=1), preferred_element_type=jnp.float32
        ).reshape(2 * feature_rows, len(pieces), head_width)
        return pair_sum_scatter(partial, "c")

    early = 2 * 2 + 1
    early_core = core_reduced(arranged, ring_pieces[:early])
    arranged_late, early_core = lax.optimization_barrier((arranged, early_core))
    kept_early = pair_sum_scatter(early_core, "xl")
    kept_late = pair_sum_scatter(core_reduced(arranged_late, ring_pieces[early:]), "xl")
    def slot_of(index):
        return kept_early[:, index] if index < early else kept_late[:, index - early]

    received = [slot_of(0)]
    shifts = [0]
    for index in range(1, y_count):
        distance = (index + 1) // 2
        shift = -distance if index % 2 == 1 and 2 * distance < y_count else distance
        perm = [(i, (i + shift) % y_count) for i in range(y_count)]
        received.append(lax.ppermute(slot_of(index), "y", perm))
        shifts.append(shift)
    quarters = jnp.stack(received).reshape(dp_count, quarter_rows, head_width)
    source_delta = jnp.asarray([-s for s in shifts], dtype=jnp.int32)
    source_y = (y + source_delta) % y_count
    source_slot = jnp.zeros(y_count, jnp.int32).at[source_y].set(jnp.arange(y_count, dtype=jnp.int32))
    block = jnp.arange(dp_count, dtype=jnp.int32)
    block_at = source_slot[block // pair_blocks] * pair_blocks + block % pair_blocks
    in_owner_order = jnp.take(quarters, block_at[inverse[0]], axis=0)
    from_all = lax.all_to_all(in_owner_order, DP, split_axis=0, concat_axis=0, tiled=True)
    own_block = jnp.sum(
        from_all.reshape(z_count, dp_count // z_count, quarter_rows, head_width), axis=0
    ).reshape(block_rows, heads_here, head_width)

    previous = momentum.reshape(block_rows, heads_here, head_width)
    new_momentum = decay_rate * previous + own_block
    nesterov = own_block + decay_rate * new_momentum
    ortho = orthogonalize(nesterov)
    own_update = (
        (ortho * math.sqrt(block_rows))
        .astype(jnp.bfloat16)
        .reshape(block_rows, heads_here * head_width)
    )
    gathered = lax.all_to_all(
        jnp.broadcast_to(own_update[None], (z_count,) + own_update.shape),
        "z",
        split_axis=0,
        concat_axis=0,
        tiled=True,
    ).reshape(z_count * block_rows, heads_here * head_width)
    gathered = pair_gather(gathered, "xl")
    partner = lax.ppermute(gathered, "c", SWAP)
    d = jnp.arange(dp_count, dtype=jnp.int32)
    update_position = (
        jnp.where(d % 2 == c, 0, half) + jnp.where((d // 2) % 2 == xl, 0, quarter) + d // 4
    )
    source = update_position[owners[0]]
    slots = jnp.arange(half, dtype=jnp.int32)[None, :]
    pick_own = (source[:, None] == slots).astype(jnp.bfloat16)
    pick_partner = (source[:, None] == slots + half).astype(jnp.bfloat16)
    block_shape = (half, block_rows, heads_here * head_width)
    placed = (
        jnp.einsum(
            "bk,krc->brc", pick_own, gathered.reshape(block_shape), preferred_element_type=jnp.float32
        )
        + jnp.einsum(
            "bk,krc->brc", pick_partner, partner.reshape(block_shape), preferred_element_type=jnp.float32
        )
    ).astype(jnp.bfloat16)
    return (
        placed.reshape(dp_count * block_rows, heads_here * head_width),
        new_momentum.reshape(block_rows, heads_here * head_width),
    )


def solution(mesh):
    dp_size, tp_size = mesh.shape["dp"], mesh.shape["tensor"]
    fine = Mesh(mesh.devices.reshape(dp_size // 4, 2, 2, tp_size // 2, 2), DP + TP)
    in_specs = (
        P(TP, DP),
        P(DP, TP),
        P(DP),
        P(DP),
        P(),
        P(TP, None),
        P(DP, TP),
    )
    out_specs = (P(None, TP), P(DP, TP))
    return jax.shard_map(shards, mesh=fine, in_specs=in_specs, out_specs=out_specs, check_vma=False)
```

```python
import math

import jax
import jax.numpy as jnp
from jax import lax
from jax.sharding import Mesh, PartitionSpec as P

ITERS = 5


decay_rate = 0.95
quintic_first = 3.4445
quintic_second = -4.775
quintic_third = 2.0315
norm_epsilon = 1e-07

DP = ("z", "xl", "c")
TP = ("y", "xh")
SWAP = [(0, 1), (1, 0)]


def token_factor(labels, diff_mask, class_weight, total_tokens):
    classes = jnp.arange(class_weight.shape[0], dtype=jnp.int32)
    picked = (labels[:, None] == classes[None, :]).astype(jnp.float32)
    token_weight = diff_mask.astype(jnp.float32) * jnp.sum(picked * class_weight[None, :], axis=1)
    return token_weight / math.sqrt(total_tokens)


def weigh(cotangents, factor):
    return (cotangents.astype(jnp.float32) * factor[:, None]).astype(jnp.bfloat16)


def invert(owners):
    number = owners.shape[1]
    candidates = jnp.arange(number, dtype=jnp.int32)
    matches = owners[:, None, :] == candidates[None, :, None]
    return jnp.sum(jnp.where(matches, candidates[None, None, :], 0), axis=2)


def reorder(blocks, lookup):
    return jnp.take_along_axis(blocks, jnp.transpose(lookup)[:, None, :, None], axis=0)


def orthogonalize(nesterov):
    frobenius = jnp.sqrt(jnp.sum(nesterov * nesterov, axis=(-3, -1), keepdims=True)) + norm_epsilon
    iterate = nesterov / frobenius
    for step in range(ITERS):
        gram_matrix = jnp.einsum(
            "...rhc,...rhd->...hcd", iterate, iterate, precision=lax.Precision.HIGHEST
        )
        poly_matrix = quintic_second * gram_matrix + quintic_third * jnp.einsum(
            "...hcd,...hde->...hce", gram_matrix, gram_matrix, precision=lax.Precision.HIGHEST
        )
        iterate = quintic_first * iterate + jnp.einsum(
            "...rhc,...hcd->...rhd", iterate, poly_matrix, precision=lax.Precision.HIGHEST
        )
    return iterate


def pair_sum_scatter(blocks, axis):
    half = blocks.shape[0] // 2
    return blocks[:half] + lax.ppermute(blocks[half:], axis, SWAP)


def xor_sum_scatter(blocks, axis, distance):
    half = blocks.shape[0] // 2
    count = lax.axis_size(axis)
    perm = [(i, i ^ distance) for i in range(count)]
    return blocks[:half] + lax.ppermute(blocks[half:], axis, perm)


def xor_gather(piece, axis, distance):
    count = lax.axis_size(axis)
    perm = [(i, i ^ distance) for i in range(count)]
    return jnp.concatenate([piece, lax.ppermute(piece, axis, perm)], axis=0)


def ring_gather(piece, axis):
    count = lax.axis_size(axis)
    to_right = [(i, (i + 1) % count) for i in range(count)]
    to_left = [(i, (i - 1) % count) for i in range(count)]
    pieces = [piece]
    from_left = from_right = piece
    for step in range(1, count // 2 + 1):
        from_left = lax.ppermute(from_left, axis, to_right)
        pieces.append(from_left)
        if 2 * step < count:
            from_right = lax.ppermute(from_right, axis, to_left)
            pieces.append(from_right)
    return pieces


def pair_gather(piece, axis):
    return jnp.concatenate([piece, lax.ppermute(piece, axis, SWAP)], axis=0)


def shards(features, cotangents, labels, diff_mask, class_weight, owners, momentum):
    dp_count = lax.axis_size(DP)
    z_count = lax.axis_size("z")
    tensor_count = lax.axis_size(TP)
    local_tokens = cotangents.shape[0]
    factor = token_factor(labels, diff_mask, class_weight, local_tokens * dp_count)
    heads_here = owners.shape[0]
    head_width = cotangents.shape[1] // heads_here
    feature_rows = features.shape[0]
    block_rows = feature_rows * tensor_count // dp_count
    sub_blocks = feature_rows // block_rows
    inverse = invert(owners)
    z = lax.axis_index("z")
    xl = lax.axis_index("xl")
    c = lax.axis_index("c")
    xh = lax.axis_index("xh")

    y_count = lax.axis_size("y")
    half, quarter = dp_count // 2, dp_count // 4
    quarter_rows = block_rows // 4
    pair_rows = pair_gather(features, "xh")
    y = lax.axis_index("y")
    ring_pieces = ring_gather(weigh(cotangents, factor), "y")
    pair_blocks = 2 * sub_blocks
    group_rows = pair_blocks * quarter_rows
    position = jnp.arange(2 * feature_rows, dtype=jnp.int32)
    group = position // group_rows
    within = position % group_rows
    j = within // quarter_rows
    r = within % quarter_rows
    quarter_xl = jnp.where(group % 2 == 0, xl, 1 - xl)
    quarter_c = jnp.where(group < 2, c, 1 - c)
    u = 2 * quarter_xl + quarter_c
    shard_slot = jnp.where(j // sub_blocks == xh, 0, 1)
    source_row = shard_slot * feature_rows + (j % sub_blocks) * block_rows + u * quarter_rows + r
    arranged = jnp.take(pair_rows, source_row, axis=0)

    def core_reduced(rows, pieces):
        partial = jnp.dot(
            rows, jnp.concatenate(pieces, axis=1), preferred_element_type=jnp.float32
        ).reshape(2 * feature_rows, len(pieces), head_width)
        return pair_sum_scatter(partial, "c")

    early = 2 * 2 + 1
    early_core = core_reduced(arranged, ring_pieces[:early])
    arranged_late, early_core = lax.optimization_barrier((arranged, early_core))
    kept_ring_order = jnp.concatenate(
        [
            pair_sum_scatter(early_core, "xl"),
            pair_sum_scatter(core_reduced(arranged_late, ring_pieces[early:]), "xl"),
        ],
        axis=1,
    )
    head = jnp.arange(y_count, dtype=jnp.int32)
    ahead = (head - y) % y_count
    behind = (y - head) % y_count
    slot = jnp.where(ahead == 0, 0, jnp.where(ahead < behind, 2 * ahead, 2 * behind - 1))
    kept = jnp.take(kept_ring_order, slot, axis=1)
    quarters = lax.all_to_all(kept, "y", split_axis=1, concat_axis=0, tiled=True).reshape(
        dp_count, quarter_rows, head_width
    )
    in_owner_order = jnp.take(quarters, inverse[0], axis=0)
    from_all = lax.all_to_all(in_owner_order, DP, split_axis=0, concat_axis=0, tiled=True)
    own_block = jnp.sum(
        from_all.reshape(z_count, dp_count // z_count, quarter_rows, head_width), axis=0
    ).reshape(block_rows, heads_here, head_width)

    previous = momentum.reshape(block_rows, heads_here, head_width)
    new_momentum = decay_rate * previous + own_block
    nesterov = own_block + decay_rate * new_momentum
    ortho = orthogonalize(nesterov)
    own_update = (
        (ortho * math.sqrt(block_rows))
        .astype(jnp.bfloat16)
        .reshape(block_rows, heads_here * head_width)
    )
    gathered = lax.all_to_all(
        jnp.broadcast_to(own_update[None], (z_count,) + own_update.shape),
        "z",
        split_axis=0,
        concat_axis=0,
        tiled=True,
    ).reshape(z_count * block_rows, heads_here * head_width)
    gathered = pair_gather(gathered, "xl")
    partner = lax.ppermute(gathered, "c", SWAP)
    d = jnp.arange(dp_count, dtype=jnp.int32)
    update_position = (
        jnp.where(d % 2 == c, 0, half) + jnp.where((d // 2) % 2 == xl, 0, quarter) + d // 4
    )
    source = update_position[owners[0]]
    slots = jnp.arange(half, dtype=jnp.int32)[None, :]
    pick_own = (source[:, None] == slots).astype(jnp.bfloat16)
    pick_partner = (source[:, None] == slots + half).astype(jnp.bfloat16)
    block_shape = (half, block_rows, heads_here * head_width)
    placed = (
        jnp.einsum(
            "bk,krc->brc", pick_own, gathered.reshape(block_shape), preferred_element_type=jnp.float32
        )
        + jnp.einsum(
            "bk,krc->brc", pick_partner, partner.reshape(block_shape), preferred_element_type=jnp.float32
        )
    ).astype(jnp.bfloat16)
    return (
        placed.reshape(dp_count * block_rows, heads_here * head_width),
        new_momentum.reshape(block_rows, heads_here * head_width),
    )


def solution(mesh):
    dp_size, tp_size = mesh.shape["dp"], mesh.shape["tensor"]
    fine = Mesh(mesh.devices.reshape(dp_size // 4, 2, 2, tp_size // 2, 2), DP + TP)
    in_specs = (
        P(TP, DP),
        P(DP, TP),
        P(DP),
        P(DP),
        P(),
        P(TP, None),
        P(DP, TP),
    )
    out_specs = (P(None, TP), P(DP, TP))
    return jax.shard_map(shards, mesh=fine, in_specs=in_specs, out_specs=out_specs, check_vma=False)
```

```python
import math

import jax
import jax.numpy as jnp
from jax import lax
from jax.sharding import Mesh, PartitionSpec as P

ITERS = 5


decay_rate = 0.95
quintic_first = 3.4445
quintic_second = -4.775
quintic_third = 2.0315
norm_epsilon = 1e-07

DP = ("z", "xl", "c")
TP = ("y", "xh")
SWAP = [(0, 1), (1, 0)]


def token_factor(labels, diff_mask, class_weight, total_tokens):
    classes = jnp.arange(class_weight.shape[0], dtype=jnp.int32)
    picked = (labels[:, None] == classes[None, :]).astype(jnp.float32)
    token_weight = diff_mask.astype(jnp.float32) * jnp.sum(picked * class_weight[None, :], axis=1)
    return token_weight / math.sqrt(total_tokens)


def weigh(cotangents, factor):
    return (cotangents.astype(jnp.float32) * factor[:, None]).astype(jnp.bfloat16)


def invert(owners):
    number = owners.shape[1]
    candidates = jnp.arange(number, dtype=jnp.int32)
    matches = owners[:, None, :] == candidates[None, :, None]
    return jnp.sum(jnp.where(matches, candidates[None, None, :], 0), axis=2)


def reorder(blocks, lookup):
    return jnp.take_along_axis(blocks, jnp.transpose(lookup)[:, None, :, None], axis=0)


def orthogonalize(nesterov):
    frobenius = jnp.sqrt(jnp.sum(nesterov * nesterov, axis=(-3, -1), keepdims=True)) + norm_epsilon
    iterate = nesterov / frobenius
    for step in range(ITERS):
        gram_matrix = jnp.einsum(
            "...rhc,...rhd->...hcd", iterate, iterate, precision=lax.Precision.HIGHEST
        )
        poly_matrix = quintic_second * gram_matrix + quintic_third * jnp.einsum(
            "...hcd,...hde->...hce", gram_matrix, gram_matrix, precision=lax.Precision.HIGHEST
        )
        iterate = quintic_first * iterate + jnp.einsum(
            "...rhc,...hcd->...rhd", iterate, poly_matrix, precision=lax.Precision.HIGHEST
        )
    return iterate


def pair_sum_scatter(blocks, axis):
    half = blocks.shape[0] // 2
    return blocks[:half] + lax.ppermute(blocks[half:], axis, SWAP)


def xor_sum_scatter(blocks, axis, distance):
    half = blocks.shape[0] // 2
    count = lax.axis_size(axis)
    perm = [(i, i ^ distance) for i in range(count)]
    return blocks[:half] + lax.ppermute(blocks[half:], axis, perm)


def xor_gather(piece, axis, distance):
    count = lax.axis_size(axis)
    perm = [(i, i ^ distance) for i in range(count)]
    return jnp.concatenate([piece, lax.ppermute(piece, axis, perm)], axis=0)


def ring_gather(piece, axis):
    count = lax.axis_size(axis)
    to_right = [(i, (i + 1) % count) for i in range(count)]
    to_left = [(i, (i - 1) % count) for i in range(count)]
    pieces = [piece]
    from_left = from_right = piece
    for step in range(1, count // 2 + 1):
        from_left = lax.ppermute(from_left, axis, to_right)
        pieces.append(from_left)
        if 2 * step < count:
            from_right = lax.ppermute(from_right, axis, to_left)
            pieces.append(from_right)
    return pieces


def pair_gather(piece, axis):
    return jnp.concatenate([piece, lax.ppermute(piece, axis, SWAP)], axis=0)


def shards(features, cotangents, labels, diff_mask, class_weight, owners, momentum):
    dp_count = lax.axis_size(DP)
    z_count = lax.axis_size("z")
    tensor_count = lax.axis_size(TP)
    local_tokens = cotangents.shape[0]
    factor = token_factor(labels, diff_mask, class_weight, local_tokens * dp_count)
    heads_here = owners.shape[0]
    head_width = cotangents.shape[1] // heads_here
    feature_rows = features.shape[0]
    block_rows = feature_rows * tensor_count // dp_count
    sub_blocks = feature_rows // block_rows
    inverse = invert(owners)
    z = lax.axis_index("z")
    xl = lax.axis_index("xl")
    c = lax.axis_index("c")
    xh = lax.axis_index("xh")

    y_count = lax.axis_size("y")
    half, quarter = dp_count // 2, dp_count // 4
    quarter_rows = block_rows // 4
    pair_rows = pair_gather(features, "xh")
    y = lax.axis_index("y")
    ring_pieces = [weigh(piece, factor) for piece in ring_gather(cotangents, "y")]
    pair_blocks = 2 * sub_blocks
    group_rows = pair_blocks * quarter_rows
    position = jnp.arange(2 * feature_rows, dtype=jnp.int32)
    group = position // group_rows
    within = position % group_rows
    j = within // quarter_rows
    r = within % quarter_rows
    quarter_xl = jnp.where(group % 2 == 0, xl, 1 - xl)
    quarter_c = jnp.where(group < 2, c, 1 - c)
    u = 2 * quarter_xl + quarter_c
    shard_slot = jnp.where(j // sub_blocks == xh, 0, 1)
    source_row = shard_slot * feature_rows + (j % sub_blocks) * block_rows + u * quarter_rows + r
    arranged = jnp.take(pair_rows, source_row, axis=0)

    def core_reduced(rows, pieces):
        partial = jnp.dot(
            rows, jnp.concatenate(pieces, axis=1), preferred_element_type=jnp.float32
        ).reshape(2 * feature_rows, len(pieces), head_width)
        return pair_sum_scatter(partial, "c")

    early = 2 * 2 + 1
    early_core = core_reduced(arranged, ring_pieces[:early])
    arranged_late, early_core = lax.optimization_barrier((arranged, early_core))
    kept_ring_order = jnp.concatenate(
        [
            pair_sum_scatter(early_core, "xl"),
            pair_sum_scatter(core_reduced(arranged_late, ring_pieces[early:]), "xl"),
        ],
        axis=1,
    )
    head = jnp.arange(y_count, dtype=jnp.int32)
    ahead = (head - y) % y_count
    behind = (y - head) % y_count
    slot = jnp.where(ahead == 0, 0, jnp.where(ahead < behind, 2 * ahead, 2 * behind - 1))
    kept = jnp.take(kept_ring_order, slot, axis=1)
    quarters = lax.all_to_all(kept, "y", split_axis=1, concat_axis=0, tiled=True).reshape(
        dp_count, quarter_rows, head_width
    )
    in_owner_order = jnp.take(quarters, inverse[0], axis=0)
    from_all = lax.all_to_all(in_owner_order, DP, split_axis=0, concat_axis=0, tiled=True)
    own_block = jnp.sum(
        from_all.reshape(z_count, dp_count // z_count, quarter_rows, head_width), axis=0
    ).reshape(block_rows, heads_here, head_width)

    previous = momentum.reshape(block_rows, heads_here, head_width)
    new_momentum = decay_rate * previous + own_block
    nesterov = own_block + decay_rate * new_momentum
    ortho = orthogonalize(nesterov)
    own_update = (
        (ortho * math.sqrt(block_rows))
        .astype(jnp.bfloat16)
        .reshape(block_rows, heads_here * head_width)
    )
    gathered = lax.all_to_all(
        jnp.broadcast_to(own_update[None], (z_count,) + own_update.shape),
        "z",
        split_axis=0,
        concat_axis=0,
        tiled=True,
    ).reshape(z_count * block_rows, heads_here * head_width)
    from_xl = lax.ppermute(gathered, "xl", SWAP)
    from_c = lax.ppermute(gathered, "c", SWAP)
    from_both = lax.ppermute(from_xl, "c", SWAP)
    source = owners[0]
    part = jnp.where((source // 2) % 2 == xl, 0, 1) + jnp.where(source % 2 == c, 0, 2)
    slots = jnp.arange(z_count, dtype=jnp.int32)[None, :]
    block_shape = (z_count, block_rows, heads_here * head_width)
    placed = sum(
        jnp.einsum(
            "bk,krc->brc",
            ((part[:, None] == index) & (source[:, None] // 4 == slots)).astype(jnp.bfloat16),
            blocks.reshape(block_shape),
            preferred_element_type=jnp.float32,
        )
        for index, blocks in enumerate((gathered, from_xl, from_c, from_both))
    ).astype(jnp.bfloat16)
    return (
        placed.reshape(dp_count * block_rows, heads_here * head_width),
        new_momentum.reshape(block_rows, heads_here * head_width),
    )


def solution(mesh):
    dp_size, tp_size = mesh.shape["dp"], mesh.shape["tensor"]
    fine = Mesh(mesh.devices.reshape(dp_size // 4, 2, 2, tp_size // 2, 2), DP + TP)
    in_specs = (
        P(TP, DP),
        P(DP, TP),
        P(DP),
        P(DP),
        P(),
        P(TP, None),
        P(DP, TP),
    )
    out_specs = (P(None, TP), P(DP, TP))
    return jax.shard_map(shards, mesh=fine, in_specs=in_specs, out_specs=out_specs, check_vma=False)
```
